32 devices in a mesh: seq: 4 (over y, x), fsdp: 8 (over z, core).
Axes of the slice: x: 2, y: 2, z: 4, core: 2. Of those that a mesh axis runs over, the one named last changes fastest.
Arguments:
- queries: bfloat16 [8, 2048, 2560], P('fsdp', 'seq'), may hold values from -26 to 26
- kv_cache: bfloat16 [8, 5, 4, 2, 128, 2560], P('fsdp', None, 'seq'), may hold values from -24 to 24
- block_lists: int32 [8, 16, 5], P('fsdp', 'seq'), may hold values from 0 to 19, as said below
- key_limit: int32 [8, 16], P('fsdp', 'seq'), may hold values from 800 to 2559, as said below
- out_weight: bfloat16 [2560, 2560], P('fsdp'), may hold values from -0.125 to 0.125
- gate: float32 [8, 2560], P('fsdp'), may hold values from -8 to 8
Outputs:
- branch: bfloat16 [8, 2048, 2560], P('fsdp', 'seq')
The draws below stay inside these ranges and needn't reach their ends.
Inputs may be any that keep to these rules, and one draw needn't show every extreme that they name: `block_lists`: in every tile's list the first 2 entries are the same distinct blocks below 4 for all tiles of a clip; the other 3 entries are consecutive blocks at or above 4, the most recent blocks before the tile's own position, and the last device's last tile reads block 19. Among the window blocks listed by the tiles of one device no two have the same remainder modulo 4. key_limit[n, t] lies 128 // 4 to 127 positions after the first position of the last block in the tile's list (the tile sees that far into its own stretch).
All inputs are finite; a program needn't handle non-finite values.
Results may differ from the reference program's by a relative error of at most 0.0058.
Values may be sent and summed in bfloat16 or wider, within the bound.
No kernel may reach another device: no remote copies, remote signals or barrier semaphores. Data moves between devices by JAX's collectives and lax.ppermute only.
A program may use at most 192 MiB of HBM per device.

```python
import math
import jax
import jax.numpy as jnp
from jax import lax

HEADS = 20
HS = 128
DOUT = 2560
BLK = 128
NSINK = 2
NWIN = 3
SINKPOOL = 4
CB = 5
HD = 2560
LIST = 5
TILES_DEV = 4
TILES = 16
QTOK = 2048
NBLK = 20
CLIPS = 8
N_SEQ = 4


def list_parts(key):
    base = jax.random.fold_in(key, 7)
    sink_key, start_key, limit_key = jax.random.split(base, 3)
    sink_keys = jax.random.split(sink_key, CLIPS)
    sinks = jax.vmap(lambda one_key: jax.random.permutation(one_key, SINKPOOL)[:NSINK])(sink_keys).astype(jnp.int32)
    sinks = sinks.at[0].set(jnp.arange(NSINK, dtype=jnp.int32))
    starts = jax.random.randint(start_key, (CLIPS, N_SEQ), SINKPOOL, NBLK - NWIN, dtype=jnp.int32)
    starts = jnp.sort(starts, axis=1).astype(jnp.int32)
    starts = starts.at[:, 0].set(SINKPOOL)
    starts = starts.at[:, N_SEQ - 1].set(NBLK - NWIN - 1)
    tile_ids = jnp.arange(TILES, dtype=jnp.int32)
    tile_start = starts[:, tile_ids // TILES_DEV] + jnp.minimum(tile_ids % TILES_DEV, 1)
    window = tile_start[:, :, None] + jnp.arange(NWIN, dtype=jnp.int32)[None, None, :]
    sink_cols = jnp.broadcast_to(sinks[:, None, :], (CLIPS, TILES, NSINK))
    block_ids = jnp.concatenate([sink_cols, window], axis=2).astype(jnp.int32)
    extra = jax.random.randint(limit_key, (CLIPS, TILES), BLK // 4, BLK, dtype=jnp.int32)
    extra = extra.at[:, 0].set(BLK // 4)
    extra = extra.at[:, TILES - 1].set(BLK - 1)
    limits = ((tile_start + NWIN - 1) * BLK + extra).astype(jnp.int32)
    return (block_ids, limits)


def draw_block_lists(key, part):
    return list_parts(key)[0]


def draw_key_limit(key, part):
    return list_parts(key)[1]


def draw_kv_cache(key, part):
    key_part, value_part = jax.random.split(jax.random.fold_in(key, 3), 2)
    shape = (CLIPS, NBLK, BLK, HEADS * HS)
    key_rows = jnp.clip(jax.random.normal(key_part, shape, jnp.float32), -6.0, 6.0)
    values = jnp.clip(4.0 * jax.random.normal(value_part, shape, jnp.float32), -24.0, 24.0)
    stacked = jnp.stack([key_rows, values], axis=2)
    return stacked.reshape(CLIPS, CB, N_SEQ, 2, BLK, HEADS * HS).astype(jnp.bfloat16)


def draw_queries(key, part):
    query_key = jax.random.fold_in(key, 9)
    shape = (CLIPS, QTOK, HEADS * HS)
    query_rows = jnp.clip(1.5 * jax.random.normal(query_key, shape, jnp.float32), -9.0, 9.0)
    return query_rows.astype(jnp.bfloat16)


def levels(key, shape, shards, low, high):
    gain, own = 1.0, jax.random.fold_in(key, 6)
    for axis_at, parts in shards:
        steps = jnp.exp(jax.random.uniform(jax.random.fold_in(own, axis_at), (parts,), jnp.float32, low / len(shards), high / len(shards)))
        gain = gain * jnp.repeat(steps, shape[axis_at] // parts).reshape([-1 if axis == axis_at else 1 for axis in range(len(shape))])
    return gain


def bell_draw(stream_key, shape, scale, most, cuts=(), kind=jnp.bfloat16):
    factor_of = levels(stream_key, shape, cuts, -0.22, 0.18) if cuts else 1.0
    drawn = jax.random.normal(stream_key, shape, jnp.float32) * scale * factor_of
    return jnp.minimum(jnp.maximum(drawn, -most), most).astype(kind)


def setup_inputs(seed: int = 0) -> dict:
    keys = jax.random.split(jax.random.key(seed), 7)
    return {
        "queries": draw_queries(jax.random.fold_in(keys[6], 71), 0),
        "kv_cache": draw_kv_cache(jax.random.fold_in(keys[6], 71), 0),
        "block_lists": draw_block_lists(jax.random.fold_in(keys[6], 71), 0),
        "key_limit": draw_key_limit(jax.random.fold_in(keys[6], 71), 0),
        "out_weight": bell_draw(keys[4], (HD, DOUT), HD ** -0.5, 0.125, ((0, 8),)),
        "gate": bell_draw(keys[5], (CLIPS, DOUT), 2.0, 8.0, ((0, 8),), jnp.float32),
    }


def reference(queries, kv_cache, block_lists, key_limit, out_weight, gate):

    def one_clip(items):
        query_all, cache_clip, block_ids, limit_row, gate_row = items
        blocks = cache_clip.reshape(NBLK, 2, BLK, HEADS * HS)
        picked = jnp.take(blocks, block_ids.reshape(-1), axis=0).reshape(TILES, LIST, 2, BLK, HEADS * HS)
        key_rows = picked[:, :, 0].reshape(TILES, LIST * BLK, HEADS, HS).astype(jnp.float32)
        values = picked[:, :, 1].reshape(TILES, LIST * BLK, HEADS, HS).astype(jnp.float32)
        query_rows = query_all.reshape(TILES, BLK, HEADS, HS).astype(jnp.float32)
        scores = jnp.einsum('tqhd,tkhd->thqk', query_rows, key_rows) / math.sqrt(HS)
        position = (block_ids[:, :, None] * BLK + jnp.arange(BLK, dtype=jnp.int32)[None, None, :]).reshape(TILES, LIST * BLK)
        allowed = (position < limit_row[:, None])[:, None, None, :]
        scores = jnp.where(allowed, scores, -jnp.inf)
        row_max = lax.optimization_barrier(jnp.max(scores, axis=-1, keepdims=True))
        exponent = jnp.exp(scores - row_max)
        weights = (exponent / lax.optimization_barrier(jnp.sum(exponent, axis=-1, keepdims=True))).astype(jnp.bfloat16)
        mixed_rows = jnp.einsum('thqk,tkhd->tqhd', weights.astype(jnp.float32), values).astype(jnp.bfloat16)
        mixed_rows = mixed_rows.reshape(QTOK, HEADS * HS)
        projected = jnp.dot(mixed_rows, out_weight, preferred_element_type=jnp.float32)
        return (gate_row[None, :] * projected).astype(jnp.bfloat16)
    return lax.map(one_clip, (queries, kv_cache, block_lists, key_limit, gate))
```

```python
import math

import jax
import jax.numpy as jnp
from jax import lax
from jax.experimental import pallas as pl
from jax.experimental.pallas import tpu as pltpu
from jax.sharding import PartitionSpec as P

HS = 128
NSINK = 2
GROUP = 4


def attention(slot_ids, block_ids, limits, query_rows, sink_pool, window_pool):
    rows, width = query_rows.shape
    block_len = sink_pool.shape[2]
    tiles, listed = block_ids.shape
    heads = width // HS
    group = GROUP if heads % GROUP == 0 else 1
    span = group * HS
    scale = math.sqrt(HS)

    def kernel(slot_ref, block_ref, limit_ref, q_ref, *refs):
        key_refs = refs[:listed]
        value_refs = refs[listed : 2 * listed]
        out_ref = refs[2 * listed]
        t = pl.program_id(1)
        limit = limit_ref[t]
        lane = lax.broadcasted_iota(jnp.int32, (1, block_len), 1)
        allowed = [block_ref[t, j] * block_len + lane < limit for j in range(listed)]
        for h in range(group):
            cols = slice(h * HS, (h + 1) * HS)
            q = q_ref[:, cols]
            scores = []
            for j in range(listed):
                s = lax.dot_general(
                    q,
                    key_refs[j][:, cols],
                    (((1,), (1,)), ((), ())),
                    preferred_element_type=jnp.float32,
                ) / scale
                scores.append(jnp.where(allowed[j], s, -jnp.inf))
            row_max = scores[0].max(axis=1, keepdims=True)
            for s in scores[1:]:
                row_max = jnp.maximum(row_max, s.max(axis=1, keepdims=True))
            exps = [jnp.exp(s - row_max) for s in scores]
            total = exps[0].sum(axis=1, keepdims=True)
            for e in exps[1:]:
                total = total + e.sum(axis=1, keepdims=True)
            acc = None
            for j in range(listed):
                w = (exps[j] / total).astype(jnp.bfloat16)
                part = jnp.dot(w, value_refs[j][:, cols], preferred_element_type=jnp.float32)
                acc = part if acc is None else acc + part
            out_ref[:, cols] = acc.astype(out_ref.dtype)

    def pool_spec(j, kv):
        def index(g, t, slot_ref, block_ref, limit_ref):
            return (slot_ref[t, j], kv, 0, g)

        return pl.BlockSpec((None, None, block_len, span), index)

    q_spec = pl.BlockSpec((block_len, span), lambda g, t, *_: (t, g))
    in_specs = [q_spec]
    operands = [query_rows]
    for kv in range(2):
        for j in range(listed):
            in_specs.append(pool_spec(j, kv))
            operands.append(sink_pool if j < NSINK else window_pool)
    grid_spec = pltpu.PrefetchScalarGridSpec(
        num_scalar_prefetch=3,
        grid=(heads // group, tiles),
        in_specs=in_specs,
        out_specs=pl.BlockSpec((block_len, span), lambda g, t, *_: (t, g)),
    )
    flops = 4 * tiles * block_len * listed * block_len * width
    cost = pl.CostEstimate(
        flops=flops,
        transcendentals=tiles * heads * block_len * listed * block_len,
        bytes_accessed=2 * rows * width * 2 + 2 * tiles * listed * block_len * width * 2,
    )
    return pl.pallas_call(
        kernel,
        grid_spec=grid_spec,
        out_shape=jax.ShapeDtypeStruct((rows, width), jnp.bfloat16),
        compiler_params=pltpu.CompilerParams(dimension_semantics=("arbitrary", "arbitrary")),
        cost_estimate=cost,
    )(slot_ids, block_ids, limits, query_rows, *operands[1:])


def shards(queries, kv_cache, block_lists, key_limit, out_weight, gate):
    owners = lax.axis_size("seq")
    me = lax.axis_index("seq")
    blocks = kv_cache[0, :, 0]
    block_ids = block_lists[0]
    tiles = block_ids.shape[0]
    block_len = blocks.shape[2]
    width = blocks.shape[3]
    weight = lax.all_gather(out_weight, "fsdp", axis=0, tiled=True)
    every_list = lax.all_gather(block_ids, "seq")
    sink_pool = lax.all_gather(blocks[0], "seq")
    readers_ids = every_list[:, :, NSINK:].reshape(owners, -1)
    asked = jnp.max(jnp.where(readers_ids % owners == me, readers_ids, -1), axis=1)
    asked_slot = jnp.maximum(asked, 0) // owners
    outgoing = jnp.take(blocks, asked_slot, axis=0)
    window_pool = lax.all_to_all(outgoing, "seq", split_axis=0, concat_axis=0, tiled=True)
    slot_ids = jnp.concatenate(
        [block_ids[:, :NSINK], block_ids[:, NSINK:] % owners], axis=1
    ).astype(jnp.int32)
    mixed = attention(
        slot_ids, block_ids, key_limit[0], queries[0], sink_pool, window_pool
    )
    projected = jnp.dot(mixed, weight, preferred_element_type=jnp.float32)
    return (gate[0][None, :] * projected).astype(jnp.bfloat16)[None]


def solution(mesh):
    in_specs = (
        P("fsdp", "seq", None),
        P("fsdp", None, "seq", None, None, None),
        P("fsdp", "seq", None),
        P("fsdp", "seq"),
        P("fsdp", None),
        P("fsdp", None),
    )
    out_specs = P("fsdp", "seq", None)
    return jax.shard_map(shards, mesh=mesh, in_specs=in_specs, out_specs=out_specs, check_vma=False)
```

```python
import math

import jax
import jax.numpy as jnp
from jax import lax
from jax.experimental import pallas as pl
from jax.experimental.pallas import tpu as pltpu
from jax.sharding import PartitionSpec as P

HS = 128
NSINK = 2
GROUP = 4


def attention(slot_ids, block_ids, limits, query_rows, sink_pool, window_pool):
    rows, width = query_rows.shape
    block_len = sink_pool.shape[2]
    tiles, listed = block_ids.shape
    heads = width // HS
    group = GROUP if heads % GROUP == 0 else 1
    span = group * HS
    inv_scale = 1.0 / math.sqrt(HS)

    def kernel(slot_ref, block_ref, limit_ref, q_ref, *refs):
        key_refs = refs[:listed]
        value_refs = refs[listed : 2 * listed]
        out_ref = refs[2 * listed]
        t = pl.program_id(1)
        limit = limit_ref[t]
        lane = lax.broadcasted_iota(jnp.int32, (1, block_len), 1)
        last = listed - 1
        allowed = block_ref[t, last] * block_len + lane < limit
        for h in range(group):
            cols = slice(h * HS, (h + 1) * HS)
            q = q_ref[:, cols]
            scores = []
            for j in range(listed):
                s = lax.dot_general(
                    q,
                    key_refs[j][:, cols],
                    (((1,), (1,)), ((), ())),
                    preferred_element_type=jnp.float32,
                ) * inv_scale
                if j == last:
                    s = jnp.where(allowed, s, -jnp.inf)
                scores.append(s)
            row_max = scores[0].max(axis=1, keepdims=True)
            for s in scores[1:]:
                row_max = jnp.maximum(row_max, s.max(axis=1, keepdims=True))
            exps = [jnp.exp(s - row_max) for s in scores]
            total = exps[0].sum(axis=1, keepdims=True)
            for e in exps[1:]:
                total = total + e.sum(axis=1, keepdims=True)
            inv_total = 1.0 / total
            acc = None
            for j in range(listed):
                w = (exps[j] * inv_total).astype(jnp.bfloat16)
                part = jnp.dot(w, value_refs[j][:, cols], preferred_element_type=jnp.float32)
                acc = part if acc is None else acc + part
            out_ref[:, cols] = acc.astype(out_ref.dtype)

    def pool_spec(j, kv):
        def index(g, t, slot_ref, block_ref, limit_ref):
            return (slot_ref[t, j], kv, 0, g)

        return pl.BlockSpec((None, None, block_len, span), index)

    q_spec = pl.BlockSpec((block_len, span), lambda g, t, *_: (t, g))
    in_specs = [q_spec]
    operands = [query_rows]
    for kv in range(2):
        for j in range(listed):
            in_specs.append(pool_spec(j, kv))
            operands.append(sink_pool if j < NSINK else window_pool)
    grid_spec = pltpu.PrefetchScalarGridSpec(
        num_scalar_prefetch=3,
        grid=(heads // group, tiles),
        in_specs=in_specs,
        out_specs=pl.BlockSpec((block_len, span), lambda g, t, *_: (t, g)),
    )
    flops = 4 * tiles * block_len * listed * block_len * width
    cost = pl.CostEstimate(
        flops=flops,
        transcendentals=tiles * heads * block_len * listed * block_len,
        bytes_accessed=2 * rows * width * 2 + 2 * tiles * listed * block_len * width * 2,
    )
    return pl.pallas_call(
        kernel,
        grid_spec=grid_spec,
        out_shape=jax.ShapeDtypeStruct((rows, width), jnp.bfloat16),
        compiler_params=pltpu.CompilerParams(dimension_semantics=("arbitrary", "arbitrary")),
        cost_estimate=cost,
    )(slot_ids, block_ids, limits, query_rows, *operands[1:])


def swap(block, owners, bit):
    return lax.ppermute(block, "seq", [(s, s ^ bit) for s in range(owners)])


def spread_sinks(own, sinks, owners, me):
    if owners != 4:
        return lax.all_gather(own, "seq"), sinks
    first = swap(own, owners, 1)
    pair = me // 2
    in_pair = sinks // 2 == pair
    count = jnp.sum(in_pair.astype(jnp.int32))
    lone = jnp.where(in_pair[0], sinks[0], sinks[1])
    relay = jnp.where((count == 1) & (lone != me), first, own)
    second = swap(relay, owners, 2)
    third = swap(second, owners, 1)
    other_count = jnp.sum((sinks // 2 != pair).astype(jnp.int32))
    slots = jnp.where(
        sinks == me,
        0,
        jnp.where(
            sinks == (me ^ 1),
            1,
            jnp.where((other_count == 1) | (sinks == (me ^ 2)), 2, 3),
        ),
    ).astype(jnp.int32)
    return jnp.stack([own, first, second, third]), slots


def shards(queries, kv_cache, block_lists, key_limit, out_weight, gate):
    owners = lax.axis_size("seq")
    me = lax.axis_index("seq")
    blocks = kv_cache[0, :, 0]
    block_ids = block_lists[0]
    tiles = block_ids.shape[0]
    block_len = blocks.shape[2]
    width = blocks.shape[3]
    weight = lax.all_gather(out_weight, "fsdp", axis=0, tiled=True)
    every_list = lax.all_gather(block_ids, "seq")
    sink_pool, sink_slots = spread_sinks(blocks[0], block_ids[0, :NSINK], owners, me)
    readers_ids = every_list[:, :, NSINK:].reshape(owners, -1)
    asked = jnp.max(jnp.where(readers_ids % owners == me, readers_ids, -1), axis=1)
    asked_slot = jnp.maximum(asked, 0) // owners
    outgoing = jnp.take(blocks, asked_slot, axis=0, mode="clip")
    window_pool = lax.all_to_all(outgoing, "seq", split_axis=0, concat_axis=0, tiled=True)
    slot_ids = jnp.concatenate(
        [jnp.broadcast_to(sink_slots[None, :], (tiles, NSINK)), block_ids[:, NSINK:] % owners],
        axis=1,
    ).astype(jnp.int32)
    mixed = attention(
        slot_ids, block_ids, key_limit[0], queries[0], sink_pool, window_pool
    )
    projected = jnp.dot(mixed, weight, preferred_element_type=jnp.float32)
    return (gate[0][None, :] * projected).astype(jnp.bfloat16)[None]


def solution(mesh):
    in_specs = (
        P("fsdp", "seq", None),
        P("fsdp", None, "seq", None, None, None),
        P("fsdp", "seq", None),
        P("fsdp", "seq"),
        P("fsdp", None),
        P("fsdp", None),
    )
    out_specs = P("fsdp", "seq", None)
    return jax.shard_map(shards, mesh=mesh, in_specs=in_specs, out_specs=out_specs, check_vma=False)
```

```python
import math

import jax
import jax.numpy as jnp
from jax import lax
from jax.experimental import pallas as pl
from jax.experimental.pallas import tpu as pltpu
from jax.sharding import PartitionSpec as P

HS = 128
NSINK = 2
GROUP = 4


def attention(slot_ids, block_ids, limits, query_rows, sink_pool, window_pool):
    rows, width = query_rows.shape
    block_len = sink_pool.shape[2]
    tiles, listed = block_ids.shape
    heads = width // HS
    group = GROUP if heads % GROUP == 0 else 1
    span = group * HS
    inv_scale = 1.0 / math.sqrt(HS)

    def kernel(slot_ref, block_ref, limit_ref, q_ref, *refs):
        key_refs = refs[:listed]
        value_refs = refs[listed : 2 * listed]
        out_ref = refs[2 * listed]
        t = pl.program_id(1)
        limit = limit_ref[t]
        lane = lax.broadcasted_iota(jnp.int32, (1, block_len), 1)
        last = listed - 1
        allowed = block_ref[t, last] * block_len + lane < limit
        for h in range(group):
            cols = slice(h * HS, (h + 1) * HS)
            q = q_ref[:, cols]
            scores = []
            for j in range(listed):
                s = lax.dot_general(
                    q,
                    key_refs[j][:, cols],
                    (((1,), (1,)), ((), ())),
                    preferred_element_type=jnp.float32,
                ) * inv_scale
                if j == last:
                    s = jnp.where(allowed, s, -jnp.inf)
                scores.append(s)
            peak = scores[0]
            for s in scores[1:]:
                peak = jnp.maximum(peak, s)
            row_max = peak.max(axis=1, keepdims=True)
            exps = [jnp.exp(s - row_max) for s in scores]
            mass = exps[0]
            for e in exps[1:]:
                mass = mass + e
            total = mass.sum(axis=1, keepdims=True)
            inv_total = 1.0 / total
            acc = None
            for j in range(listed):
                w = (exps[j] * inv_total).astype(jnp.bfloat16)
                part = jnp.dot(w, value_refs[j][:, cols], preferred_element_type=jnp.float32)
                acc = part if acc is None else acc + part
            out_ref[:, cols] = acc.astype(out_ref.dtype)

    def pool_spec(j, kv):
        def index(g, t, slot_ref, block_ref, limit_ref):
            return (slot_ref[t, j], kv, 0, g)

        return pl.BlockSpec((None, None, block_len, span), index)

    q_spec = pl.BlockSpec((block_len, span), lambda g, t, *_: (t, g))
    in_specs = [q_spec]
    operands = [query_rows]
    for kv in range(2):
        for j in range(listed):
            in_specs.append(pool_spec(j, kv))
            operands.append(sink_pool if j < NSINK else window_pool)
    grid_spec = pltpu.PrefetchScalarGridSpec(
        num_scalar_prefetch=3,
        grid=(heads // group, tiles),
        in_specs=in_specs,
        out_specs=pl.BlockSpec((block_len, span), lambda g, t, *_: (t, g)),
    )
    flops = 4 * tiles * block_len * listed * block_len * width
    cost = pl.CostEstimate(
        flops=flops,
        transcendentals=tiles * heads * block_len * listed * block_len,
        bytes_accessed=2 * rows * width * 2 + 2 * tiles * listed * block_len * width * 2,
    )
    return pl.pallas_call(
        kernel,
        grid_spec=grid_spec,
        out_shape=jax.ShapeDtypeStruct((rows, width), jnp.bfloat16),
        compiler_params=pltpu.CompilerParams(dimension_semantics=("arbitrary", "arbitrary")),
        cost_estimate=cost,
    )(slot_ids, block_ids, limits, query_rows, *operands[1:])


def swap(block, owners, bit):
    return lax.ppermute(block, "seq", [(s, s ^ bit) for s in range(owners)])


def spread_sinks(own, sinks, owners, me):
    if owners != 4:
        return lax.all_gather(own, "seq"), sinks
    first = swap(own, owners, 1)
    pair = me // 2
    in_pair = sinks // 2 == pair
    count = jnp.sum(in_pair.astype(jnp.int32))
    lone = jnp.where(in_pair[0], sinks[0], sinks[1])
    relay = jnp.where((count == 1) & (lone != me), first, own)
    second = swap(relay, owners, 2)
    third = swap(second, owners, 1)
    other_count = jnp.sum((sinks // 2 != pair).astype(jnp.int32))
    slots = jnp.where(
        sinks == me,
        0,
        jnp.where(
            sinks == (me ^ 1),
            1,
            jnp.where((other_count == 1) | (sinks == (me ^ 2)), 2, 3),
        ),
    ).astype(jnp.int32)
    return jnp.stack([own, first, second, third]), slots


def shards(queries, kv_cache, block_lists, key_limit, out_weight, gate):
    owners = lax.axis_size("seq")
    me = lax.axis_index("seq")
    blocks = kv_cache[0, :, 0]
    block_ids = block_lists[0]
    tiles = block_ids.shape[0]
    block_len = blocks.shape[2]
    width = blocks.shape[3]
    weight = lax.all_gather(out_weight, "fsdp", axis=0, tiled=True)
    every_list = lax.all_gather(block_ids, "seq")
    every_list, blocks = lax.optimization_barrier((every_list, blocks))
    sink_pool, sink_slots = spread_sinks(blocks[0], block_ids[0, :NSINK], owners, me)
    readers_ids = every_list[:, :, NSINK:].reshape(owners, -1)
    asked = jnp.max(jnp.where(readers_ids % owners == me, readers_ids, -1), axis=1)
    asked_slot = jnp.maximum(asked, 0) // owners
    outgoing = jnp.take(blocks, asked_slot, axis=0, mode="clip")
    window_pool = lax.all_to_all(outgoing, "seq", split_axis=0, concat_axis=0, tiled=True)
    slot_ids = jnp.concatenate(
        [jnp.broadcast_to(sink_slots[None, :], (tiles, NSINK)), block_ids[:, NSINK:] % owners],
        axis=1,
    ).astype(jnp.int32)
    mixed = attention(
        slot_ids, block_ids, key_limit[0], queries[0], sink_pool, window_pool
    )
    projected = jnp.dot(mixed, weight, preferred_element_type=jnp.float32)
    return (gate[0][None, :] * projected).astype(jnp.bfloat16)[None]


def solution(mesh):
    in_specs = (
        P("fsdp", "seq", None),
        P("fsdp", None, "seq", None, None, None),
        P("fsdp", "seq", None),
        P("fsdp", "seq"),
        P("fsdp", None),
        P("fsdp", None),
    )
    out_specs = P("fsdp", "seq", None)
    return jax.shard_map(shards, mesh=mesh, in_specs=in_specs, out_specs=out_specs, check_vma=False)
```

```python
import math

import jax
import jax.numpy as jnp
from jax import lax
from jax.experimental import pallas as pl
from jax.experimental.pallas import tpu as pltpu
from jax.sharding import PartitionSpec as P

HS = 128
NSINK = 2
GROUP = 4


def attention(sink_slots, bias, query_rows, sink_pool, window_pool):
    rows, width = query_rows.shape
    block_len = sink_pool.shape[2]
    owners = window_pool.shape[0]
    pooled = NSINK + owners
    heads = width // HS
    group = GROUP if heads % GROUP == 0 else 1
    span = group * HS
    inv_scale = 1.0 / math.sqrt(HS)

    def kernel(slot_ref, bias_ref, q_ref, *refs):
        key_refs = refs[:pooled]
        value_refs = refs[pooled : 2 * pooled]
        out_ref = refs[2 * pooled]
        mask = bias_ref[...]
        for h in range(group):
            cols = slice(h * HS, (h + 1) * HS)
            keys = jnp.concatenate([r[:, cols] for r in key_refs], axis=0)
            values = jnp.concatenate([r[:, cols] for r in value_refs], axis=0)
            s = lax.dot_general(
                q_ref[:, cols], keys, (((1,), (1,)), ((), ())), preferred_element_type=jnp.float32
            )
            s = s * inv_scale + mask
            row_max = s.max(axis=1, keepdims=True)
            e = jnp.exp(s - row_max)
            inv_total = 1.0 / e.sum(axis=1, keepdims=True)
            w = (e * inv_total).astype(jnp.bfloat16)
            out_ref[:, cols] = jnp.dot(w, values, preferred_element_type=jnp.float32).astype(
                out_ref.dtype
            )

    def sink_spec(u, kv):
        return pl.BlockSpec(
            (None, None, block_len, span), lambda g, slot_ref: (slot_ref[u], kv, 0, g)
        )

    def window_spec(r, kv):
        return pl.BlockSpec((None, None, block_len, span), lambda g, slot_ref: (r, kv, 0, g))

    in_specs = [
        pl.BlockSpec((rows, pooled * block_len), lambda g, slot_ref: (0, 0)),
        pl.BlockSpec((rows, span), lambda g, slot_ref: (0, g)),
    ]
    operands = [bias, query_rows]
    for kv in range(2):
        for u in range(NSINK):
            in_specs.append(sink_spec(u, kv))
            operands.append(sink_pool)
        for r in range(owners):
            in_specs.append(window_spec(r, kv))
            operands.append(window_pool)
    grid_spec = pltpu.PrefetchScalarGridSpec(
        num_scalar_prefetch=1,
        grid=(heads // group,),
        in_specs=in_specs,
        out_specs=pl.BlockSpec((rows, span), lambda g, slot_ref: (0, g)),
    )
    keys_total = pooled * block_len
    cost = pl.CostEstimate(
        flops=4 * rows * keys_total * width,
        transcendentals=heads * rows * keys_total,
        bytes_accessed=2 * rows * width * 2 + 2 * keys_total * width * 2 + rows * keys_total * 4,
    )
    return pl.pallas_call(
        kernel,
        grid_spec=grid_spec,
        out_shape=jax.ShapeDtypeStruct((rows, width), jnp.bfloat16),
        compiler_params=pltpu.CompilerParams(dimension_semantics=("arbitrary",)),
        cost_estimate=cost,
    )(sink_slots, *operands)


def visibility(block_ids, limits, owners, block_len):
    tiles = block_ids.shape[0]
    sinks = block_ids[:, :NSINK]
    window = block_ids[:, NSINK:]
    match = window[:, :, None] % owners == jnp.arange(owners, dtype=jnp.int32)[None, None, :]
    held = jnp.max(jnp.where(match, window[:, :, None], -1), axis=1)
    pooled_ids = jnp.concatenate([sinks, held], axis=1)
    visible = jnp.where(
        pooled_ids >= 0, jnp.clip(limits[:, None] - pooled_ids * block_len, 0, block_len), 0
    )
    lane = jnp.arange(block_len, dtype=jnp.int32)
    seen = lane[None, None, :] < visible[:, :, None]
    bias = jnp.where(seen, 0.0, -jnp.inf).astype(jnp.float32)
    bias = bias.reshape(tiles, 1, -1)
    return jnp.broadcast_to(bias, (tiles, block_len, bias.shape[-1])).reshape(
        tiles * block_len, -1
    )


def swap(block, owners, bit):
    return lax.ppermute(block, "seq", [(s, s ^ bit) for s in range(owners)])


def spread_sinks(own, sinks, owners, me):
    if owners != 4:
        return lax.all_gather(own, "seq"), sinks
    first = swap(own, owners, 1)
    pair = me // 2
    in_pair = sinks // 2 == pair
    count = jnp.sum(in_pair.astype(jnp.int32))
    lone = jnp.where(in_pair[0], sinks[0], sinks[1])
    relay = jnp.where((count == 1) & (lone != me), first, own)
    second = swap(relay, owners, 2)
    third = swap(second, owners, 1)
    other_count = jnp.sum((sinks // 2 != pair).astype(jnp.int32))
    slots = jnp.where(
        sinks == me,
        0,
        jnp.where(
            sinks == (me ^ 1),
            1,
            jnp.where((other_count == 1) | (sinks == (me ^ 2)), 2, 3),
        ),
    ).astype(jnp.int32)
    return jnp.stack([own, first, second, third]), slots


def shards(queries, kv_cache, block_lists, key_limit, out_weight, gate):
    owners = lax.axis_size("seq")
    me = lax.axis_index("seq")
    blocks = kv_cache[0, :, 0]
    block_ids = block_lists[0]
    tiles = block_ids.shape[0]
    block_len = blocks.shape[2]
    width = blocks.shape[3]
    weight = lax.all_gather(out_weight, "fsdp", axis=0, tiled=True)
    every_list = lax.all_gather(block_ids, "seq")
    every_list, blocks = lax.optimization_barrier((every_list, blocks))
    sink_pool, sink_slots = spread_sinks(blocks[0], block_ids[0, :NSINK], owners, me)
    readers_ids = every_list[:, :, NSINK:].reshape(owners, -1)
    asked = jnp.max(jnp.where(readers_ids % owners == me, readers_ids, -1), axis=1)
    asked_slot = jnp.maximum(asked, 0) // owners
    outgoing = jnp.take(blocks, asked_slot, axis=0, mode="clip")
    window_pool = lax.all_to_all(outgoing, "seq", split_axis=0, concat_axis=0, tiled=True)
    bias = visibility(block_ids, key_limit[0], owners, block_len)
    mixed = attention(sink_slots, bias, queries[0], sink_pool, window_pool)
    projected = jnp.dot(mixed, weight, preferred_element_type=jnp.float32)
    return (gate[0][None, :] * projected).astype(jnp.bfloat16)[None]


def solution(mesh):
    in_specs = (
        P("fsdp", "seq", None),
        P("fsdp", None, "seq", None, None, None),
        P("fsdp", "seq", None),
        P("fsdp", "seq"),
        P("fsdp", None),
        P("fsdp", None),
    )
    out_specs = P("fsdp", "seq", None)
    return jax.shard_map(shards, mesh=mesh, in_specs=in_specs, out_specs=out_specs, check_vma=False)
```

```python
import math

import jax
import jax.numpy as jnp
from jax import lax
from jax.experimental import pallas as pl
from jax.experimental.pallas import tpu as pltpu
from jax.sharding import PartitionSpec as P

HS = 128
NSINK = 2
GROUP = 4


def attention(sink_ids, bias, query_rows, arrived):
    rows, width = query_rows.shape
    block_len = arrived.shape[3]
    owners = arrived.shape[0]
    pooled = NSINK + owners
    heads = width // HS
    group = GROUP if heads % GROUP == 0 else 1
    span = group * HS
    inv_scale = 1.0 / math.sqrt(HS)

    def kernel(slot_ref, bias_ref, q_ref, *refs):
        key_refs = refs[:pooled]
        value_refs = refs[pooled : 2 * pooled]
        out_ref = refs[2 * pooled]
        mask = bias_ref[...]
        for h in range(group):
            cols = slice(h * HS, (h + 1) * HS)
            keys = jnp.concatenate([r[:, cols] for r in key_refs], axis=0)
            values = jnp.concatenate([r[:, cols] for r in value_refs], axis=0)
            s = lax.dot_general(
                q_ref[:, cols], keys, (((1,), (1,)), ((), ())), preferred_element_type=jnp.float32
            )
            s = s * inv_scale + mask
            row_max = s.max(axis=1, keepdims=True)
            e = jnp.exp(s - row_max)
            inv_total = 1.0 / e.sum(axis=1, keepdims=True)
            w = (e * inv_total).astype(jnp.bfloat16)
            out_ref[:, cols] = jnp.dot(w, values, preferred_element_type=jnp.float32).astype(
                out_ref.dtype
            )

    def sink_spec(u, kv):
        return pl.BlockSpec(
            (None, None, None, block_len, span), lambda g, slot_ref: (slot_ref[u], 1, kv, 0, g)
        )

    def window_spec(r, kv):
        return pl.BlockSpec(
            (None, None, None, block_len, span), lambda g, slot_ref: (r, 0, kv, 0, g)
        )

    in_specs = [
        pl.BlockSpec((rows, pooled * block_len), lambda g, slot_ref: (0, 0)),
        pl.BlockSpec((rows, span), lambda g, slot_ref: (0, g)),
    ]
    operands = [bias, query_rows]
    for kv in range(2):
        for u in range(NSINK):
            in_specs.append(sink_spec(u, kv))
            operands.append(arrived)
        for r in range(owners):
            in_specs.append(window_spec(r, kv))
            operands.append(arrived)
    grid_spec = pltpu.PrefetchScalarGridSpec(
        num_scalar_prefetch=1,
        grid=(heads // group,),
        in_specs=in_specs,
        out_specs=pl.BlockSpec((rows, span), lambda g, slot_ref: (0, g)),
    )
    keys_total = pooled * block_len
    cost = pl.CostEstimate(
        flops=4 * rows * keys_total * width,
        transcendentals=heads * rows * keys_total,
        bytes_accessed=2 * rows * width * 2 + 2 * keys_total * width * 2 + rows * keys_total * 4,
    )
    return pl.pallas_call(
        kernel,
        grid_spec=grid_spec,
        out_shape=jax.ShapeDtypeStruct((rows, width), jnp.bfloat16),
        compiler_params=pltpu.CompilerParams(dimension_semantics=("arbitrary",)),
        cost_estimate=cost,
    )(sink_ids, *operands)


def visibility(block_ids, limits, owners, block_len):
    tiles = block_ids.shape[0]
    sinks = block_ids[:, :NSINK]
    window = block_ids[:, NSINK:]
    match = window[:, :, None] % owners == jnp.arange(owners, dtype=jnp.int32)[None, None, :]
    held = jnp.max(jnp.where(match, window[:, :, None], -1), axis=1)
    pooled_ids = jnp.concatenate([sinks, held], axis=1)
    visible = jnp.where(
        pooled_ids >= 0, jnp.clip(limits[:, None] - pooled_ids * block_len, 0, block_len), 0
    )
    lane = jnp.arange(block_len, dtype=jnp.int32)
    seen = lane[None, None, :] < visible[:, :, None]
    bias = jnp.where(seen, 0.0, -jnp.inf).astype(jnp.float32)
    bias = bias.reshape(tiles, 1, -1)
    return jnp.broadcast_to(bias, (tiles, block_len, bias.shape[-1])).reshape(
        tiles * block_len, -1
    )


def shards(queries, kv_cache, block_lists, key_limit, out_weight, gate):
    owners = lax.axis_size("seq")
    me = lax.axis_index("seq")
    blocks = kv_cache[0, :, 0]
    block_ids = block_lists[0]
    tiles = block_ids.shape[0]
    block_len = blocks.shape[2]
    width = blocks.shape[3]
    weight = lax.all_gather(out_weight, "fsdp", axis=0, tiled=True)
    every_list = lax.all_gather(block_ids, "seq")
    readers_ids = every_list[:, :, NSINK:].reshape(owners, -1)
    asked = jnp.max(jnp.where(readers_ids % owners == me, readers_ids, -1), axis=1)
    asked_slot = jnp.maximum(asked, 0) // owners
    wanted = jnp.take(blocks, asked_slot, axis=0, mode="clip")
    first = jnp.broadcast_to(blocks[0][None], wanted.shape)
    outgoing = jnp.stack([wanted, first], axis=1)
    arrived = lax.all_to_all(outgoing, "seq", split_axis=0, concat_axis=0, tiled=True)
    bias = visibility(block_ids, key_limit[0], owners, block_len)
    mixed = attention(block_ids[0, :NSINK], bias, queries[0], arrived)
    projected = jnp.dot(mixed, weight, preferred_element_type=jnp.float32)
    return (gate[0][None, :] * projected).astype(jnp.bfloat16)[None]


def solution(mesh):
    in_specs = (
        P("fsdp", "seq", None),
        P("fsdp", None, "seq", None, None, None),
        P("fsdp", "seq", None),
        P("fsdp", "seq"),
        P("fsdp", None),
        P("fsdp", None),
    )
    out_specs = P("fsdp", "seq", None)
    return jax.shard_map(shards, mesh=mesh, in_specs=in_specs, out_specs=out_specs, check_vma=False)
```

```python
import math

import jax
import jax.numpy as jnp
from jax import lax
from jax.experimental import pallas as pl
from jax.experimental.pallas import tpu as pltpu
from jax.sharding import PartitionSpec as P

HS = 128
NSINK = 2
GROUPS = (5, 4, 2, 1)
CHUNKS = 2


def attention(sink_ids, bias, query_rows, arrived, chunk):
    rows = query_rows.shape[0]
    width = arrived.shape[-1]
    block_len = arrived.shape[3]
    owners = arrived.shape[0]
    pooled = NSINK + owners
    heads = width // HS
    group = next(g for g in GROUPS if heads % g == 0)
    span = group * HS
    inv_scale = 1.0 / math.sqrt(HS)

    def kernel(slot_ref, bias_ref, q_ref, *refs):
        key_refs = refs[:pooled]
        value_refs = refs[pooled : 2 * pooled]
        out_ref = refs[2 * pooled]
        mask = bias_ref[...]
        for h in range(group):
            cols = slice(h * HS, (h + 1) * HS)
            keys = jnp.concatenate([r[:, cols] for r in key_refs], axis=0)
            values = jnp.concatenate([r[:, cols] for r in value_refs], axis=0)
            s = lax.dot_general(
                q_ref[:, cols], keys, (((1,), (1,)), ((), ())), preferred_element_type=jnp.float32
            )
            s = s * inv_scale + mask
            row_max = s.max(axis=1, keepdims=True)
            e = jnp.exp(s - row_max)
            inv_total = 1.0 / e.sum(axis=1, keepdims=True)
            w = (e * inv_total).astype(jnp.bfloat16)
            out_ref[:, cols] = jnp.dot(w, values, preferred_element_type=jnp.float32).astype(
                out_ref.dtype
            )

    def sink_spec(u, kv):
        return pl.BlockSpec(
            (None, None, None, block_len, span), lambda g, slot_ref: (slot_ref[u], 1, kv, 0, g)
        )

    def window_spec(r, kv):
        return pl.BlockSpec(
            (None, None, None, block_len, span), lambda g, slot_ref: (r, 0, kv, 0, g)
        )

    in_specs = [
        pl.BlockSpec((rows, pooled * block_len), lambda g, slot_ref: (0, 0)),
        pl.BlockSpec((rows, span), lambda g, slot_ref: (0, g + chunk * (heads // group))),
    ]
    operands = [bias, query_rows]
    for kv in range(2):
        for u in range(NSINK):
            in_specs.append(sink_spec(u, kv))
            operands.append(arrived)
        for r in range(owners):
            in_specs.append(window_spec(r, kv))
            operands.append(arrived)
    grid_spec = pltpu.PrefetchScalarGridSpec(
        num_scalar_prefetch=1,
        grid=(heads // group,),
        in_specs=in_specs,
        out_specs=pl.BlockSpec((rows, span), lambda g, slot_ref: (0, g)),
    )
    keys_total = pooled * block_len
    cost = pl.CostEstimate(
        flops=4 * rows * keys_total * width,
        transcendentals=heads * rows * keys_total,
        bytes_accessed=2 * rows * width * 2 + 2 * keys_total * width * 2 + rows * keys_total * 4,
    )
    return pl.pallas_call(
        kernel,
        grid_spec=grid_spec,
        out_shape=jax.ShapeDtypeStruct((rows, width), jnp.bfloat16),
        compiler_params=pltpu.CompilerParams(dimension_semantics=("arbitrary",)),
        cost_estimate=cost,
    )(sink_ids, *operands)


def visibility(block_ids, limits, owners, block_len):
    tiles = block_ids.shape[0]
    sinks = block_ids[:, :NSINK]
    window = block_ids[:, NSINK:]
    match = window[:, :, None] % owners == jnp.arange(owners, dtype=jnp.int32)[None, None, :]
    held = jnp.max(jnp.where(match, window[:, :, None], -1), axis=1)
    pooled_ids = jnp.concatenate([sinks, held], axis=1)
    visible = jnp.where(
        pooled_ids >= 0, jnp.clip(limits[:, None] - pooled_ids * block_len, 0, block_len), 0
    )
    lane = jnp.arange(block_len, dtype=jnp.int32)
    seen = lane[None, None, :] < visible[:, :, None]
    bias = jnp.where(seen, 0.0, -jnp.inf).astype(jnp.float32)
    bias = bias.reshape(tiles, 1, -1)
    return jnp.broadcast_to(bias, (tiles, block_len, bias.shape[-1])).reshape(
        tiles * block_len, -1
    )


def shards(queries, kv_cache, block_lists, key_limit, out_weight, gate):
    owners = lax.axis_size("seq")
    me = lax.axis_index("seq")
    blocks = kv_cache[0, :, 0]
    block_ids = block_lists[0]
    tiles = block_ids.shape[0]
    block_len = blocks.shape[2]
    width = blocks.shape[3]
    weight = lax.all_gather(out_weight, "fsdp", axis=0, tiled=True)
    every_list = lax.all_gather(block_ids, "seq")
    readers_ids = every_list[:, :, NSINK:].reshape(owners, -1)
    asked = jnp.max(jnp.where(readers_ids % owners == me, readers_ids, -1), axis=1)
    asked_slot = jnp.maximum(asked, 0) // owners
    picks = jnp.stack([asked_slot, jnp.zeros_like(asked_slot)], axis=1).reshape(-1)
    bias = visibility(block_ids, key_limit[0], owners, block_len)
    chunks = CHUNKS if (width // HS) % CHUNKS == 0 else 1
    chunk_width = width // chunks
    projected = None
    for c in range(chunks):
        cols = slice(c * chunk_width, (c + 1) * chunk_width)
        outgoing = jnp.take(blocks[..., cols], picks, axis=0, mode="clip")
        outgoing = outgoing.reshape(owners, 2, 2, block_len, chunk_width)
        arrived = lax.all_to_all(outgoing, "seq", split_axis=0, concat_axis=0, tiled=True)
        mixed = attention(block_ids[0, :NSINK], bias, queries[0], arrived, c)
        part = jnp.dot(mixed, weight[cols], preferred_element_type=jnp.float32)
        projected = part if projected is None else projected + part
    return (gate[0][None, :] * projected).astype(jnp.bfloat16)[None]


def solution(mesh):
    in_specs = (
        P("fsdp", "seq", None),
        P("fsdp", None, "seq", None, None, None),
        P("fsdp", "seq", None),
        P("fsdp", "seq"),
        P("fsdp", None),
        P("fsdp", None),
    )
    out_specs = P("fsdp", "seq", None)
    return jax.shard_map(shards, mesh=mesh, in_specs=in_specs, out_specs=out_specs, check_vma=False)
```

```python
import math

import jax
import jax.numpy as jnp
from jax import lax
from jax.experimental import pallas as pl
from jax.experimental.pallas import tpu as pltpu
from jax.sharding import PartitionSpec as P

HS = 128
NSINK = 2
GROUPS = (5, 4, 2, 1)
CHUNKS = 4


def attention(sink_ids, bias, query_rows, arrived, chunk):
    rows = query_rows.shape[0]
    width = arrived.shape[-1]
    block_len = arrived.shape[3]
    owners = arrived.shape[0]
    pooled = NSINK + owners
    heads = width // HS
    group = next(g for g in GROUPS if heads % g == 0)
    span = group * HS
    inv_scale = 1.0 / math.sqrt(HS)

    def kernel(slot_ref, bias_ref, q_ref, *refs):
        key_refs = refs[:pooled]
        value_refs = refs[pooled : 2 * pooled]
        out_ref = refs[2 * pooled]
        mask = bias_ref[...]
        for h in range(group):
            cols = slice(h * HS, (h + 1) * HS)
            keys = jnp.concatenate([r[:, cols] for r in key_refs], axis=0)
            values = jnp.concatenate([r[:, cols] for r in value_refs], axis=0)
            s = lax.dot_general(
                q_ref[:, cols], keys, (((1,), (1,)), ((), ())), preferred_element_type=jnp.float32
            )
            s = s * inv_scale + mask
            row_max = s.max(axis=1, keepdims=True)
            e = jnp.exp(s - row_max)
            inv_total = 1.0 / e.sum(axis=1, keepdims=True)
            w = (e * inv_total).astype(jnp.bfloat16)
            out_ref[:, cols] = jnp.dot(w, values, preferred_element_type=jnp.float32).astype(
                out_ref.dtype
            )

    def sink_spec(u, kv):
        return pl.BlockSpec(
            (None, None, None, block_len, span), lambda g, slot_ref: (slot_ref[u], 1, kv, 0, g)
        )

    def window_spec(r, kv):
        return pl.BlockSpec(
            (None, None, None, block_len, span), lambda g, slot_ref: (r, 0, kv, 0, g)
        )

    in_specs = [
        pl.BlockSpec((rows, pooled * block_len), lambda g, slot_ref: (0, 0)),
        pl.BlockSpec((rows, span), lambda g, slot_ref: (0, g + chunk * (heads // group))),
    ]
    operands = [bias, query_rows]
    for kv in range(2):
        for u in range(NSINK):
            in_specs.append(sink_spec(u, kv))
            operands.append(arrived)
        for r in range(owners):
            in_specs.append(window_spec(r, kv))
            operands.append(arrived)
    grid_spec = pltpu.PrefetchScalarGridSpec(
        num_scalar_prefetch=1,
        grid=(heads // group,),
        in_specs=in_specs,
        out_specs=pl.BlockSpec((rows, span), lambda g, slot_ref: (0, g)),
    )
    keys_total = pooled * block_len
    cost = pl.CostEstimate(
        flops=4 * rows * keys_total * width,
        transcendentals=heads * rows * keys_total,
        bytes_accessed=2 * rows * width * 2 + 2 * keys_total * width * 2 + rows * keys_total * 4,
    )
    return pl.pallas_call(
        kernel,
        grid_spec=grid_spec,
        out_shape=jax.ShapeDtypeStruct((rows, width), jnp.bfloat16),
        compiler_params=pltpu.CompilerParams(dimension_semantics=("arbitrary",)),
        cost_estimate=cost,
    )(sink_ids, *operands)


def pack(slots, blocks, chunk, chunk_width):
    owners = slots.shape[0]
    _, pair, block_len, _ = blocks.shape
    offset = chunk * chunk_width

    def kernel(slot_ref, blocks_ref, out_ref, sems):
        copies = []
        for r in range(owners):
            for k in range(2):
                source = slot_ref[r] if k == 0 else 0
                copy = pltpu.make_async_copy(
                    blocks_ref.at[source, :, :, pl.ds(offset, chunk_width)],
                    out_ref.at[r, k],
                    sems.at[r, k],
                )
                copy.start()
                copies.append(copy)
        for copy in copies:
            copy.wait()

    return pl.pallas_call(
        kernel,
        grid_spec=pltpu.PrefetchScalarGridSpec(
            num_scalar_prefetch=1,
            grid=(1,),
            in_specs=[pl.BlockSpec(memory_space=pl.ANY)],
            out_specs=pl.BlockSpec(memory_space=pl.ANY),
            scratch_shapes=[pltpu.SemaphoreType.DMA((owners, 2))],
        ),
        out_shape=jax.ShapeDtypeStruct(
            (owners, 2, pair, block_len, chunk_width), blocks.dtype
        ),
    )(slots, blocks)


def visibility(block_ids, limits, owners, block_len):
    tiles = block_ids.shape[0]
    sinks = block_ids[:, :NSINK]
    window = block_ids[:, NSINK:]
    match = window[:, :, None] % owners == jnp.arange(owners, dtype=jnp.int32)[None, None, :]
    held = jnp.max(jnp.where(match, window[:, :, None], -1), axis=1)
    pooled_ids = jnp.concatenate([sinks, held], axis=1)
    visible = jnp.where(
        pooled_ids >= 0, jnp.clip(limits[:, None] - pooled_ids * block_len, 0, block_len), 0
    )
    lane = jnp.arange(block_len, dtype=jnp.int32)
    seen = lane[None, None, :] < visible[:, :, None]
    bias = jnp.where(seen, 0.0, -jnp.inf).astype(jnp.float32)
    bias = bias.reshape(tiles, 1, -1)
    return jnp.broadcast_to(bias, (tiles, block_len, bias.shape[-1])).reshape(
        tiles * block_len, -1
    )


def shards(queries, kv_cache, block_lists, key_limit, out_weight, gate):
    owners = lax.axis_size("seq")
    me = lax.axis_index("seq")
    blocks = kv_cache[0, :, 0]
    block_ids = block_lists[0]
    tiles = block_ids.shape[0]
    block_len = blocks.shape[2]
    width = blocks.shape[3]
    weight = lax.all_gather(out_weight, "fsdp", axis=0, tiled=True)
    every_list = lax.all_gather(block_ids, "seq")
    readers_ids = every_list[:, :, NSINK:].reshape(owners, -1)
    asked = jnp.max(jnp.where(readers_ids % owners == me, readers_ids, -1), axis=1)
    asked_slot = jnp.maximum(asked, 0) // owners
    asked_slot = jnp.minimum(asked_slot, blocks.shape[0] - 1).astype(jnp.int32)
    bias = visibility(block_ids, key_limit[0], owners, block_len)
    chunks = CHUNKS if (width // HS) % CHUNKS == 0 else 1
    chunk_width = width // chunks
    projected = None
    for c in range(chunks):
        cols = slice(c * chunk_width, (c + 1) * chunk_width)
        outgoing = pack(asked_slot, blocks, c, chunk_width)
        arrived = lax.all_to_all(outgoing, "seq", split_axis=0, concat_axis=0, tiled=True)
        mixed = attention(block_ids[0, :NSINK], bias, queries[0], arrived, c)
        part = jnp.dot(mixed, weight[cols], preferred_element_type=jnp.float32)
        projected = part if projected is None else projected + part
    return (gate[0][None, :] * projected).astype(jnp.bfloat16)[None]


def solution(mesh):
    in_specs = (
        P("fsdp", "seq", None),
        P("fsdp", None, "seq", None, None, None),
        P("fsdp", "seq", None),
        P("fsdp", "seq"),
        P("fsdp", None),
        P("fsdp", None),
    )
    out_specs = P("fsdp", "seq", None)
    return jax.shard_map(shards, mesh=mesh, in_specs=in_specs, out_specs=out_specs, check_vma=False)
```

```python
import math

import jax
import jax.numpy as jnp
from jax import lax
from jax.experimental import pallas as pl
from jax.experimental.pallas import tpu as pltpu
from jax.sharding import PartitionSpec as P

HS = 128
NSINK = 2
GROUPS = (5, 4, 2, 1)
CHUNKS = 2


def attention(sink_slots, bias, query_rows, candidates, arrived, chunk):
    rows = query_rows.shape[0]
    owners, _, block_len, width = arrived.shape
    held = len(candidates)
    pooled = NSINK + owners
    heads = width // HS
    group = next(g for g in GROUPS if heads % g == 0)
    span = group * HS
    steps = heads // group
    inv_scale = 1.0 / math.sqrt(HS)

    def kernel(slot_ref, bias_ref, q_ref, *refs):
        cand_refs = refs[: 2 * held]
        window_refs = refs[2 * held : 2 * held + 2 * owners]
        out_ref = refs[2 * held + 2 * owners]
        mask = bias_ref[...]
        for h in range(group):
            cols = slice(h * HS, (h + 1) * HS)
            pools = []
            for kv in range(2):
                parts = []
                for u in range(NSINK):
                    pick = cand_refs[kv * held][:, cols]
                    for i in range(1, held):
                        pick = jnp.where(slot_ref[u] == i, cand_refs[kv * held + i][:, cols], pick)
                    parts.append(pick)
                for r in range(owners):
                    parts.append(window_refs[kv * owners + r][:, cols])
                pools.append(jnp.concatenate(parts, axis=0))
            keys, values = pools
            s = lax.dot_general(
                q_ref[:, cols], keys, (((1,), (1,)), ((), ())), preferred_element_type=jnp.float32
            )
            s = s * inv_scale + mask
            row_max = s.max(axis=1, keepdims=True)
            e = jnp.exp(s - row_max)
            inv_total = 1.0 / e.sum(axis=1, keepdims=True)
            w = (e * inv_total).astype(jnp.bfloat16)
            out_ref[:, cols] = jnp.dot(w, values, preferred_element_type=jnp.float32).astype(
                out_ref.dtype
            )

    def cand_spec(kv):
        return pl.BlockSpec(
            (None, block_len, span), lambda g, slot_ref: (kv, 0, g + chunk * steps)
        )

    def window_spec(r, kv):
        return pl.BlockSpec((None, None, block_len, span), lambda g, slot_ref: (r, kv, 0, g))

    in_specs = [
        pl.BlockSpec((rows, pooled * block_len), lambda g, slot_ref: (0, 0)),
        pl.BlockSpec((rows, span), lambda g, slot_ref: (0, g + chunk * steps)),
    ]
    operands = [bias, query_rows]
    for kv in range(2):
        for cand in candidates:
            in_specs.append(cand_spec(kv))
            operands.append(cand)
    for kv in range(2):
        for r in range(owners):
            in_specs.append(window_spec(r, kv))
            operands.append(arrived)
    grid_spec = pltpu.PrefetchScalarGridSpec(
        num_scalar_prefetch=1,
        grid=(steps,),
        in_specs=in_specs,
        out_specs=pl.BlockSpec((rows, span), lambda g, slot_ref: (0, g)),
    )
    keys_total = pooled * block_len
    cost = pl.CostEstimate(
        flops=4 * rows * keys_total * width,
        transcendentals=heads * rows * keys_total,
        bytes_accessed=2 * rows * width * 2 + 2 * keys_total * width * 2 + rows * keys_total * 4,
    )
    return pl.pallas_call(
        kernel,
        grid_spec=grid_spec,
        out_shape=jax.ShapeDtypeStruct((rows, width), jnp.bfloat16),
        compiler_params=pltpu.CompilerParams(dimension_semantics=("arbitrary",)),
        cost_estimate=cost,
    )(sink_slots, *operands)


def swap(block, owners, bit):
    return lax.ppermute(block, "seq", [(s, s ^ bit) for s in range(owners)])


def spread_sinks(own, sinks, owners, me):
    if owners != 4:
        pool = lax.all_gather(own, "seq")
        picked = [lax.dynamic_index_in_dim(pool, sinks[u], 0, False) for u in range(NSINK)]
        return picked, jnp.arange(NSINK, dtype=jnp.int32)
    first = swap(own, owners, 1)
    pair = me // 2
    in_pair = sinks // 2 == pair
    count = jnp.sum(in_pair.astype(jnp.int32))
    lone = jnp.where(in_pair[0], sinks[0], sinks[1])
    relay = jnp.where((count == 1) & (lone != me), first, own)
    second = swap(relay, owners, 2)
    third = swap(second, owners, 1)
    other_count = jnp.sum((sinks // 2 != pair).astype(jnp.int32))
    slots = jnp.where(
        sinks == me,
        0,
        jnp.where(
            sinks == (me ^ 1),
            1,
            jnp.where((other_count == 1) | (sinks == (me ^ 2)), 2, 3),
        ),
    ).astype(jnp.int32)
    return [own, first, second, third], slots


def visibility(block_ids, limits, owners, block_len):
    tiles = block_ids.shape[0]
    sinks = block_ids[:, :NSINK]
    window = block_ids[:, NSINK:]
    match = window[:, :, None] % owners == jnp.arange(owners, dtype=jnp.int32)[None, None, :]
    held = jnp.max(jnp.where(match, window[:, :, None], -1), axis=1)
    pooled_ids = jnp.concatenate([sinks, held], axis=1)
    visible = jnp.where(
        pooled_ids >= 0, jnp.clip(limits[:, None] - pooled_ids * block_len, 0, block_len), 0
    )
    lane = jnp.arange(block_len, dtype=jnp.int32)
    seen = lane[None, None, :] < visible[:, :, None]
    bias = jnp.where(seen, 0.0, -jnp.inf).astype(jnp.float32)
    bias = bias.reshape(tiles, 1, -1)
    return jnp.broadcast_to(bias, (tiles, block_len, bias.shape[-1])).reshape(
        tiles * block_len, -1
    )


def shards(queries, kv_cache, block_lists, key_limit, out_weight, gate):
    owners = lax.axis_size("seq")
    me = lax.axis_index("seq")
    blocks = kv_cache[0, :, 0]
    block_ids = block_lists[0]
    tiles = block_ids.shape[0]
    block_len = blocks.shape[2]
    width = blocks.shape[3]
    weight = lax.all_gather(out_weight, "fsdp", axis=0, tiled=True)
    every_list = lax.all_gather(block_ids, "seq")
    readers_ids = every_list[:, :, NSINK:].reshape(owners, -1)
    asked = jnp.max(jnp.where(readers_ids % owners == me, readers_ids, -1), axis=1)
    asked_slot = jnp.maximum(asked, 0) // owners
    candidates, sink_slots = spread_sinks(blocks[0], block_ids[0, :NSINK], owners, me)
    bias = visibility(block_ids, key_limit[0], owners, block_len)
    chunks = CHUNKS if (width // HS) % CHUNKS == 0 else 1
    chunk_width = width // chunks
    projected = None
    for c in range(chunks):
        cols = slice(c * chunk_width, (c + 1) * chunk_width)
        outgoing = jnp.take(blocks[..., cols], asked_slot, axis=0, mode="clip")
        arrived = lax.all_to_all(outgoing, "seq", split_axis=0, concat_axis=0, tiled=True)
        mixed = attention(sink_slots, bias, queries[0], candidates, arrived, c)
        part = jnp.dot(mixed, weight[cols], preferred_element_type=jnp.float32)
        projected = part if projected is None else projected + part
    return (gate[0][None, :] * projected).astype(jnp.bfloat16)[None]


def solution(mesh):
    in_specs = (
        P("fsdp", "seq", None),
        P("fsdp", None, "seq", None, None, None),
        P("fsdp", "seq", None),
        P("fsdp", "seq"),
        P("fsdp", None),
        P("fsdp", None),
    )
    out_specs = P("fsdp", "seq", None)
    return jax.shard_map(shards, mesh=mesh, in_specs=in_specs, out_specs=out_specs, check_vma=False)
```

```python
import math

import jax
import jax.numpy as jnp
from jax import lax
from jax.experimental import pallas as pl
from jax.experimental.pallas import tpu as pltpu
from jax.sharding import PartitionSpec as P

HS = 128
NSINK = 2
GROUPS = (5, 4, 2, 1)


def attention(sink_ids, bias, query_rows, arrived, col_start):
    rows = query_rows.shape[0]
    width = arrived.shape[-1]
    block_len = arrived.shape[3]
    owners = arrived.shape[0]
    pooled = NSINK + owners
    heads = width // HS
    group = next(g for g in GROUPS if heads % g == 0)
    span = group * HS
    inv_scale = 1.0 / math.sqrt(HS)

    def kernel(slot_ref, bias_ref, q_ref, *refs):
        key_refs = refs[:pooled]
        value_refs = refs[pooled : 2 * pooled]
        out_ref = refs[2 * pooled]
        mask = bias_ref[...]
        for h in range(group):
            cols = slice(h * HS, (h + 1) * HS)
            keys = jnp.concatenate([r[:, cols] for r in key_refs], axis=0)
            values = jnp.concatenate([r[:, cols] for r in value_refs], axis=0)
            s = lax.dot_general(
                q_ref[:, cols], keys, (((1,), (1,)), ((), ())), preferred_element_type=jnp.float32
            )
            s = s * inv_scale + mask
            row_max = s.max(axis=1, keepdims=True)
            e = jnp.exp(s - row_max)
            inv_total = 1.0 / e.sum(axis=1, keepdims=True)
            w = (e * inv_total).astype(jnp.bfloat16)
            out_ref[:, cols] = jnp.dot(w, values, preferred_element_type=jnp.float32).astype(
                out_ref.dtype
            )

    def sink_spec(u, kv):
        return pl.BlockSpec(
            (None, None, None, block_len, span), lambda g, slot_ref: (slot_ref[u], 1, kv, 0, g)
        )

    def window_spec(r, kv):
        return pl.BlockSpec(
            (None, None, None, block_len, span), lambda g, slot_ref: (r, 0, kv, 0, g)
        )

    in_specs = [
        pl.BlockSpec((rows, pooled * block_len), lambda g, slot_ref: (0, 0)),
        pl.BlockSpec((rows, span), lambda g, slot_ref: (0, g + col_start // span)),
    ]
    operands = [bias, query_rows]
    for kv in range(2):
        for u in range(NSINK):
            in_specs.append(sink_spec(u, kv))
            operands.append(arrived)
        for r in range(owners):
            in_specs.append(window_spec(r, kv))
            operands.append(arrived)
    grid_spec = pltpu.PrefetchScalarGridSpec(
        num_scalar_prefetch=1,
        grid=(heads // group,),
        in_specs=in_specs,
        out_specs=pl.BlockSpec((rows, span), lambda g, slot_ref: (0, g)),
    )
    keys_total = pooled * block_len
    cost = pl.CostEstimate(
        flops=4 * rows * keys_total * width,
        transcendentals=heads * rows * keys_total,
        bytes_accessed=2 * rows * width * 2 + 2 * keys_total * width * 2 + rows * keys_total * 4,
    )
    return pl.pallas_call(
        kernel,
        grid_spec=grid_spec,
        out_shape=jax.ShapeDtypeStruct((rows, width), jnp.bfloat16),
        compiler_params=pltpu.CompilerParams(dimension_semantics=("arbitrary",)),
        cost_estimate=cost,
    )(sink_ids, *operands)


def visibility(block_ids, limits, owners, block_len):
    tiles = block_ids.shape[0]
    sinks = block_ids[:, :NSINK]
    window = block_ids[:, NSINK:]
    match = window[:, :, None] % owners == jnp.arange(owners, dtype=jnp.int32)[None, None, :]
    held = jnp.max(jnp.where(match, window[:, :, None], -1), axis=1)
    pooled_ids = jnp.concatenate([sinks, held], axis=1)
    visible = jnp.where(
        pooled_ids >= 0, jnp.clip(limits[:, None] - pooled_ids * block_len, 0, block_len), 0
    )
    lane = jnp.arange(block_len, dtype=jnp.int32)
    seen = lane[None, None, :] < visible[:, :, None]
    bias = jnp.where(seen, 0.0, -jnp.inf).astype(jnp.float32)
    bias = bias.reshape(tiles, 1, -1)
    return jnp.broadcast_to(bias, (tiles, block_len, bias.shape[-1])).reshape(
        tiles * block_len, -1
    )


def shards(queries, kv_cache, block_lists, key_limit, out_weight, gate):
    owners = lax.axis_size("seq")
    me = lax.axis_index("seq")
    blocks = kv_cache[0, :, 0]
    block_ids = block_lists[0]
    tiles = block_ids.shape[0]
    block_len = blocks.shape[2]
    width = blocks.shape[3]
    weight = lax.all_gather(out_weight, "fsdp", axis=0, tiled=True)
    every_list = lax.all_gather(block_ids, "seq")
    readers_ids = every_list[:, :, NSINK:].reshape(owners, -1)
    asked = jnp.max(jnp.where(readers_ids % owners == me, readers_ids, -1), axis=1)
    asked_slot = jnp.maximum(asked, 0) // owners
    picks = jnp.stack([asked_slot, jnp.zeros_like(asked_slot)], axis=1).reshape(-1)
    bias = visibility(block_ids, key_limit[0], owners, block_len)
    heads = width // HS
    tail_heads = heads // 4 if heads % 20 == 0 else heads
    bounds = [(0, heads - tail_heads), (heads - tail_heads, heads)]
    bounds = [(lo * HS, hi * HS) for lo, hi in bounds if hi > lo]
    projected = None
    for lo, hi in bounds:
        cols = slice(lo, hi)
        outgoing = jnp.take(blocks[..., cols], picks, axis=0, mode="clip")
        outgoing = outgoing.reshape(owners, 2, 2, block_len, hi - lo)
        arrived = lax.all_to_all(outgoing, "seq", split_axis=0, concat_axis=0, tiled=True)
        if projected is not None:
            projected, arrived = lax.optimization_barrier((projected, arrived))
        mixed = attention(block_ids[0, :NSINK], bias, queries[0], arrived, lo)
        part = jnp.dot(mixed, weight[cols], preferred_element_type=jnp.float32)
        projected = part if projected is None else projected + part
    return (gate[0][None, :] * projected).astype(jnp.bfloat16)[None]


def solution(mesh):
    in_specs = (
        P("fsdp", "seq", None),
        P("fsdp", None, "seq", None, None, None),
        P("fsdp", "seq", None),
        P("fsdp", "seq"),
        P("fsdp", None),
        P("fsdp", None),
    )
    out_specs = P("fsdp", "seq", None)
    return jax.shard_map(shards, mesh=mesh, in_specs=in_specs, out_specs=out_specs, check_vma=False)
```

```python
import math

import jax
import jax.numpy as jnp
from jax import lax
from jax.experimental import pallas as pl
from jax.experimental.pallas import tpu as pltpu
from jax.sharding import PartitionSpec as P

HS = 128
NSINK = 2
GROUPS = (5, 4, 2, 1)


def attention(sink_ids, bias, query_rows, arrived, col_start):
    rows = query_rows.shape[0]
    width = arrived.shape[-1]
    block_len = arrived.shape[3]
    owners = arrived.shape[0]
    pooled = NSINK + owners
    heads = width // HS
    group = next(g for g in GROUPS if heads % g == 0)
    span = group * HS
    inv_scale = 1.0 / math.sqrt(HS)

    def kernel(slot_ref, bias_ref, q_ref, *refs):
        key_refs = refs[:pooled]
        value_refs = refs[pooled : 2 * pooled]
        out_ref = refs[2 * pooled]
        mask = bias_ref[...]
        for h in range(group):
            cols = slice(h * HS, (h + 1) * HS)
            keys = jnp.concatenate([r[:, cols] for r in key_refs], axis=0)
            values = jnp.concatenate([r[:, cols] for r in value_refs], axis=0)
            s = lax.dot_general(
                q_ref[:, cols], keys, (((1,), (1,)), ((), ())), preferred_element_type=jnp.float32
            )
            s = s * inv_scale + mask
            row_max = s.max(axis=1, keepdims=True)
            e = jnp.exp(s - row_max)
            inv_total = 1.0 / e.sum(axis=1, keepdims=True)
            w = (e * inv_total).astype(jnp.bfloat16)
            out_ref[:, cols] = jnp.dot(w, values, preferred_element_type=jnp.float32).astype(
                out_ref.dtype
            )

    def sink_spec(u, kv):
        return pl.BlockSpec(
            (None, None, None, block_len, span), lambda g, slot_ref: (slot_ref[u], 1, kv, 0, g)
        )

    def window_spec(r, kv):
        return pl.BlockSpec(
            (None, None, None, block_len, span), lambda g, slot_ref: (r, 0, kv, 0, g)
        )

    in_specs = [
        pl.BlockSpec((rows, pooled * block_len), lambda g, slot_ref: (0, 0)),
        pl.BlockSpec((rows, span), lambda g, slot_ref: (0, g + col_start // span)),
    ]
    operands = [bias, query_rows]
    for kv in range(2):
        for u in range(NSINK):
            in_specs.append(sink_spec(u, kv))
            operands.append(arrived)
        for r in range(owners):
            in_specs.append(window_spec(r, kv))
            operands.append(arrived)
    grid_spec = pltpu.PrefetchScalarGridSpec(
        num_scalar_prefetch=1,
        grid=(heads // group,),
        in_specs=in_specs,
        out_specs=pl.BlockSpec((rows, span), lambda g, slot_ref: (0, g)),
    )
    keys_total = pooled * block_len
    cost = pl.CostEstimate(
        flops=4 * rows * keys_total * width,
        transcendentals=heads * rows * keys_total,
        bytes_accessed=2 * rows * width * 2 + 2 * keys_total * width * 2 + rows * keys_total * 4,
    )
    return pl.pallas_call(
        kernel,
        grid_spec=grid_spec,
        out_shape=jax.ShapeDtypeStruct((rows, width), jnp.bfloat16),
        compiler_params=pltpu.CompilerParams(dimension_semantics=("arbitrary",)),
        cost_estimate=cost,
    )(sink_ids, *operands)


def visibility(block_ids, limits, owners, block_len):
    tiles = block_ids.shape[0]
    sinks = block_ids[:, :NSINK]
    window = block_ids[:, NSINK:]
    match = window[:, :, None] % owners == jnp.arange(owners, dtype=jnp.int32)[None, None, :]
    held = jnp.max(jnp.where(match, window[:, :, None], -1), axis=1)
    pooled_ids = jnp.concatenate([sinks, held], axis=1)
    visible = jnp.where(
        pooled_ids >= 0, jnp.clip(limits[:, None] - pooled_ids * block_len, 0, block_len), 0
    )
    lane = jnp.arange(block_len, dtype=jnp.int32)
    seen = lane[None, None, :] < visible[:, :, None]
    bias = jnp.where(seen, 0.0, -jnp.inf).astype(jnp.float32)
    bias = bias.reshape(tiles, 1, -1)
    return jnp.broadcast_to(bias, (tiles, block_len, bias.shape[-1])).reshape(
        tiles * block_len, -1
    )


def shards(queries, kv_cache, block_lists, key_limit, out_weight, gate):
    owners = lax.axis_size("seq")
    me = lax.axis_index("seq")
    blocks = kv_cache[0, :, 0]
    block_ids = block_lists[0]
    tiles = block_ids.shape[0]
    block_len = blocks.shape[2]
    width = blocks.shape[3]
    weight = lax.all_gather(out_weight, "fsdp", axis=0, tiled=True)
    window_ids = block_ids[:, NSINK:].reshape(-1)
    lists = [window_ids]
    for shift in range(1, owners):
        lists.append(lax.ppermute(window_ids, "seq", [(s, (s + shift) % owners) for s in range(owners)]))
    by_reader = jnp.stack(lists)
    readers = (me - jnp.arange(owners, dtype=jnp.int32)) % owners
    readers_ids = jnp.zeros_like(by_reader).at[readers].set(by_reader)
    asked = jnp.max(jnp.where(readers_ids % owners == me, readers_ids, -1), axis=1)
    asked_slot = jnp.minimum(jnp.maximum(asked, 0) // owners, blocks.shape[0] - 1)
    picks = jnp.stack([asked_slot, jnp.zeros_like(asked_slot)], axis=1).reshape(-1)
    bias = visibility(block_ids, key_limit[0], owners, block_len)
    heads = width // HS
    tail_heads = heads // 4 if heads % 20 == 0 else heads
    bounds = [(0, heads - tail_heads), (heads - tail_heads, heads)]
    bounds = [(lo * HS, hi * HS) for lo, hi in bounds if hi > lo]
    projected = None
    for lo, hi in bounds:
        cols = slice(lo, hi)
        outgoing = jnp.stack(
            [lax.dynamic_index_in_dim(blocks, picks[i], 0, False)[..., cols] for i in range(2 * owners)]
        ).reshape(owners, 2, 2, block_len, hi - lo)
        arrived = lax.all_to_all(outgoing, "seq", split_axis=0, concat_axis=0, tiled=True)
        if projected is not None:
            projected, arrived = lax.optimization_barrier((projected, arrived))
        mixed = attention(block_ids[0, :NSINK], bias, queries[0], arrived, lo)
        part = jnp.dot(mixed, weight[cols], preferred_element_type=jnp.float32)
        projected = part if projected is None else projected + part
    return (gate[0][None, :] * projected).astype(jnp.bfloat16)[None]


def solution(mesh):
    in_specs = (
        P("fsdp", "seq", None),
        P("fsdp", None, "seq", None, None, None),
        P("fsdp", "seq", None),
        P("fsdp", "seq"),
        P("fsdp", None),
        P("fsdp", None),
    )
    out_specs = P("fsdp", "seq", None)
    return jax.shard_map(shards, mesh=mesh, in_specs=in_specs, out_specs=out_specs, check_vma=False)
```

```python
import math

import jax
import jax.numpy as jnp
from jax import lax
from jax.experimental import pallas as pl
from jax.experimental.pallas import tpu as pltpu
from jax.sharding import PartitionSpec as P

HS = 128
NSINK = 2
GROUPS = (5, 4, 2, 1)


def attention(sink_ids, bias, query_rows, arrived, col_start):
    rows = query_rows.shape[0]
    width = arrived.shape[-1]
    block_len = arrived.shape[3]
    owners = arrived.shape[0]
    pooled = NSINK + owners
    heads = width // HS
    group = next(g for g in GROUPS if heads % g == 0)
    span = group * HS
    inv_scale = 1.0 / math.sqrt(HS)

    def kernel(slot_ref, bias_ref, q_ref, *refs):
        key_refs = refs[:pooled]
        value_refs = refs[pooled : 2 * pooled]
        out_ref = refs[2 * pooled]
        mask = bias_ref[...]
        for h in range(group):
            cols = slice(h * HS, (h + 1) * HS)
            keys = jnp.concatenate([r[:, cols] for r in key_refs], axis=0)
            values = jnp.concatenate([r[:, cols] for r in value_refs], axis=0)
            s = lax.dot_general(
                q_ref[:, cols], keys, (((1,), (1,)), ((), ())), preferred_element_type=jnp.float32
            )
            s = s * inv_scale + mask
            row_max = s.max(axis=1, keepdims=True)
            e = jnp.exp(s - row_max)
            inv_total = 1.0 / e.sum(axis=1, keepdims=True)
            w = (e * inv_total).astype(jnp.bfloat16)
            out_ref[:, cols] = jnp.dot(w, values, preferred_element_type=jnp.float32).astype(
                out_ref.dtype
            )

    def sink_spec(u, kv):
        return pl.BlockSpec(
            (None, None, None, block_len, span), lambda g, slot_ref: (slot_ref[u], 1, kv, 0, g)
        )

    def window_spec(r, kv):
        return pl.BlockSpec(
            (None, None, None, block_len, span), lambda g, slot_ref: (r, 0, kv, 0, g)
        )

    in_specs = [
        pl.BlockSpec((rows, pooled * block_len), lambda g, slot_ref: (0, 0)),
        pl.BlockSpec((rows, span), lambda g, slot_ref: (0, g + col_start // span)),
    ]
    operands = [bias, query_rows]
    for kv in range(2):
        for u in range(NSINK):
            in_specs.append(sink_spec(u, kv))
            operands.append(arrived)
        for r in range(owners):
            in_specs.append(window_spec(r, kv))
            operands.append(arrived)
    grid_spec = pltpu.PrefetchScalarGridSpec(
        num_scalar_prefetch=1,
        grid=(heads // group,),
        in_specs=in_specs,
        out_specs=pl.BlockSpec((rows, span), lambda g, slot_ref: (0, g)),
    )
    keys_total = pooled * block_len
    cost = pl.CostEstimate(
        flops=4 * rows * keys_total * width,
        transcendentals=heads * rows * keys_total,
        bytes_accessed=2 * rows * width * 2 + 2 * keys_total * width * 2 + rows * keys_total * 4,
    )
    return pl.pallas_call(
        kernel,
        grid_spec=grid_spec,
        out_shape=jax.ShapeDtypeStruct((rows, width), jnp.bfloat16),
        compiler_params=pltpu.CompilerParams(dimension_semantics=("arbitrary",)),
        cost_estimate=cost,
    )(sink_ids, *operands)


def visibility(block_ids, limits, owners, block_len):
    tiles = block_ids.shape[0]
    sinks = block_ids[:, :NSINK]
    window = block_ids[:, NSINK:]
    match = window[:, :, None] % owners == jnp.arange(owners, dtype=jnp.int32)[None, None, :]
    held = jnp.max(jnp.where(match, window[:, :, None], -1), axis=1)
    pooled_ids = jnp.concatenate([sinks, held], axis=1)
    visible = jnp.where(
        pooled_ids >= 0, jnp.clip(limits[:, None] - pooled_ids * block_len, 0, block_len), 0
    )
    lane = jnp.arange(block_len, dtype=jnp.int32)
    seen = lane[None, None, :] < visible[:, :, None]
    bias = jnp.where(seen, 0.0, -jnp.inf).astype(jnp.float32)
    bias = bias.reshape(tiles, 1, -1)
    return jnp.broadcast_to(bias, (tiles, block_len, bias.shape[-1])).reshape(
        tiles * block_len, -1
    )


def shards(queries, kv_cache, block_lists, key_limit, out_weight, gate):
    owners = lax.axis_size("seq")
    me = lax.axis_index("seq")
    blocks = kv_cache[0, :, 0]
    block_ids = block_lists[0]
    tiles = block_ids.shape[0]
    block_len = blocks.shape[2]
    width = blocks.shape[3]
    weight = lax.all_gather(out_weight, "fsdp", axis=0, tiled=True)
    window_ids = block_ids[:, NSINK:].reshape(-1)
    lists = [window_ids]
    for shift in range(1, owners):
        lists.append(lax.ppermute(window_ids, "seq", [(s, (s + shift) % owners) for s in range(owners)]))
    by_reader = jnp.stack(lists)
    readers = (me - jnp.arange(owners, dtype=jnp.int32)) % owners
    readers_ids = jnp.zeros_like(by_reader).at[readers].set(by_reader)
    asked = jnp.max(jnp.where(readers_ids % owners == me, readers_ids, -1), axis=1)
    asked_slot = jnp.minimum(jnp.maximum(asked, 0) // owners, blocks.shape[0] - 1)
    picks = jnp.stack([asked_slot, jnp.zeros_like(asked_slot)], axis=1).reshape(-1)
    bias = visibility(block_ids, key_limit[0], owners, block_len)
    heads = width // HS
    tail_heads = heads // 4 if heads % 20 == 0 else heads
    bounds = [(0, heads - tail_heads), (heads - tail_heads, heads)]
    bounds = [(lo * HS, hi * HS) for lo, hi in bounds if hi > lo]
    projected = None
    for lo, hi in bounds:
        cols = slice(lo, hi)
        outgoing = jnp.take(blocks[..., cols], picks, axis=0, mode="clip")
        outgoing = outgoing.reshape(owners, 2, 2, block_len, hi - lo)
        arrived = lax.all_to_all(outgoing, "seq", split_axis=0, concat_axis=0, tiled=True)
        if projected is not None:
            projected, arrived = lax.optimization_barrier((projected, arrived))
        mixed = attention(block_ids[0, :NSINK], bias, queries[0], arrived, lo)
        part = jnp.dot(mixed, weight[cols], preferred_element_type=jnp.float32)
        projected = part if projected is None else projected + part
    return (gate[0][None, :] * projected).astype(jnp.bfloat16)[None]


def solution(mesh):
    in_specs = (
        P("fsdp", "seq", None),
        P("fsdp", None, "seq", None, None, None),
        P("fsdp", "seq", None),
        P("fsdp", "seq"),
        P("fsdp", None),
        P("fsdp", None),
    )
    out_specs = P("fsdp", "seq", None)
    return jax.shard_map(shards, mesh=mesh, in_specs=in_specs, out_specs=out_specs, check_vma=False)
```

```python
import math

import jax
import jax.numpy as jnp
from jax import lax
from jax.experimental import pallas as pl
from jax.experimental.pallas import tpu as pltpu
from jax.sharding import PartitionSpec as P

HS = 128
NSINK = 2
GROUPS = (5, 4, 2, 1)


def attention(sink_ids, bias, query_rows, arrived, col_start):
    rows = query_rows.shape[0]
    width = arrived.shape[-1]
    block_len = arrived.shape[3]
    owners = arrived.shape[0]
    pooled = NSINK + owners
    heads = width // HS
    group = next(g for g in GROUPS if heads % g == 0)
    span = group * HS
    inv_scale = 1.0 / math.sqrt(HS)

    def kernel(slot_ref, bias_ref, q_ref, *refs):
        key_refs = refs[:pooled]
        value_refs = refs[pooled : 2 * pooled]
        out_ref = refs[2 * pooled]
        mask = bias_ref[...]
        for h in range(group):
            cols = slice(h * HS, (h + 1) * HS)
            keys = jnp.concatenate([r[:, cols] for r in key_refs], axis=0)
            values = jnp.concatenate([r[:, cols] for r in value_refs], axis=0)
            s = lax.dot_general(
                q_ref[:, cols], keys, (((1,), (1,)), ((), ())), preferred_element_type=jnp.float32
            )
            s = s * inv_scale + mask
            row_max = s.max(axis=1, keepdims=True)
            e = jnp.exp(s - row_max)
            inv_total = 1.0 / e.sum(axis=1, keepdims=True)
            w = (e * inv_total).astype(jnp.bfloat16)
            out_ref[:, cols] = jnp.dot(w, values, preferred_element_type=jnp.float32).astype(
                out_ref.dtype
            )

    def sink_spec(u, kv):
        return pl.BlockSpec(
            (None, None, None, block_len, span), lambda g, slot_ref: (slot_ref[u], 1, kv, 0, g)
        )

    def window_spec(r, kv):
        return pl.BlockSpec(
            (None, None, None, block_len, span), lambda g, slot_ref: (r, 0, kv, 0, g)
        )

    in_specs = [
        pl.BlockSpec((rows, pooled * block_len), lambda g, slot_ref: (0, 0)),
        pl.BlockSpec((rows, span), lambda g, slot_ref: (0, g + col_start // span)),
    ]
    operands = [bias, query_rows]
    for kv in range(2):
        for u in range(NSINK):
            in_specs.append(sink_spec(u, kv))
            operands.append(arrived)
        for r in range(owners):
            in_specs.append(window_spec(r, kv))
            operands.append(arrived)
    grid_spec = pltpu.PrefetchScalarGridSpec(
        num_scalar_prefetch=1,
        grid=(heads // group,),
        in_specs=in_specs,
        out_specs=pl.BlockSpec((rows, span), lambda g, slot_ref: (0, g)),
    )
    keys_total = pooled * block_len
    cost = pl.CostEstimate(
        flops=4 * rows * keys_total * width,
        transcendentals=heads * rows * keys_total,
        bytes_accessed=2 * rows * width * 2 + 2 * keys_total * width * 2 + rows * keys_total * 4,
    )
    return pl.pallas_call(
        kernel,
        grid_spec=grid_spec,
        out_shape=jax.ShapeDtypeStruct((rows, width), jnp.bfloat16),
        compiler_params=pltpu.CompilerParams(dimension_semantics=("arbitrary",)),
        cost_estimate=cost,
    )(sink_ids, *operands)


def visibility(block_ids, limits, owners, block_len):
    tiles = block_ids.shape[0]
    sinks = block_ids[:, :NSINK]
    window = block_ids[:, NSINK:]
    match = window[:, :, None] % owners == jnp.arange(owners, dtype=jnp.int32)[None, None, :]
    held = jnp.max(jnp.where(match, window[:, :, None], -1), axis=1)
    pooled_ids = jnp.concatenate([sinks, held], axis=1)
    visible = jnp.where(
        pooled_ids >= 0, jnp.clip(limits[:, None] - pooled_ids * block_len, 0, block_len), 0
    )
    lane = jnp.arange(block_len, dtype=jnp.int32)
    seen = lane[None, None, :] < visible[:, :, None]
    bias = jnp.where(seen, 0.0, -jnp.inf).astype(jnp.float32)
    bias = bias.reshape(tiles, 1, -1)
    return jnp.broadcast_to(bias, (tiles, block_len, bias.shape[-1])).reshape(
        tiles * block_len, -1
    )


def shards(queries, kv_cache, block_lists, key_limit, out_weight, gate):
    owners = lax.axis_size("seq")
    me = lax.axis_index("seq")
    blocks = kv_cache[0, :, 0]
    block_ids = block_lists[0]
    tiles = block_ids.shape[0]
    block_len = blocks.shape[2]
    width = blocks.shape[3]
    weight = lax.all_gather(out_weight, "fsdp", axis=0, tiled=True)
    window_ids = block_ids[:, NSINK:].reshape(-1)
    lists = [window_ids]
    for shift in range(1, owners):
        lists.append(lax.ppermute(window_ids, "seq", [(s, (s + shift) % owners) for s in range(owners)]))
    by_reader = jnp.stack(lists)
    readers = (me - jnp.arange(owners, dtype=jnp.int32)) % owners
    readers_ids = jnp.zeros_like(by_reader).at[readers].set(by_reader)
    asked = jnp.max(jnp.where(readers_ids % owners == me, readers_ids, -1), axis=1)
    asked_slot = jnp.minimum(jnp.maximum(asked, 0) // owners, blocks.shape[0] - 1)
    picks = jnp.stack([asked_slot, jnp.zeros_like(asked_slot)], axis=1).reshape(-1)
    bias = visibility(block_ids, key_limit[0], owners, block_len)
    heads = width // HS
    if heads % 10 == 0:
        edges = [0, heads * 6 // 10, heads * 9 // 10, heads]
    else:
        edges = [0, heads]
    bounds = [(lo * HS, hi * HS) for lo, hi in zip(edges[:-1], edges[1:])]
    projected = None
    for lo, hi in bounds:
        cols = slice(lo, hi)
        outgoing = jnp.take(blocks[..., cols], picks, axis=0, mode="clip")
        outgoing = outgoing.reshape(owners, 2, 2, block_len, hi - lo)
        arrived = lax.all_to_all(outgoing, "seq", split_axis=0, concat_axis=0, tiled=True)
        if hi == bounds[-1][1] and projected is not None:
            projected, arrived = lax.optimization_barrier((projected, arrived))
        mixed = attention(block_ids[0, :NSINK], bias, queries[0], arrived, lo)
        part = jnp.dot(mixed, weight[cols], preferred_element_type=jnp.float32)
        projected = part if projected is None else projected + part
    return (gate[0][None, :] * projected).astype(jnp.bfloat16)[None]


def solution(mesh):
    in_specs = (
        P("fsdp", "seq", None),
        P("fsdp", None, "seq", None, None, None),
        P("fsdp", "seq", None),
        P("fsdp", "seq"),
        P("fsdp", None),
        P("fsdp", None),
    )
    out_specs = P("fsdp", "seq", None)
    return jax.shard_map(shards, mesh=mesh, in_specs=in_specs, out_specs=out_specs, check_vma=False)
```

```python
import math

import jax
import jax.numpy as jnp
from jax import lax
from jax.experimental import pallas as pl
from jax.experimental.pallas import tpu as pltpu
from jax.sharding import PartitionSpec as P

HS = 128
NSINK = 2
GROUPS = (5, 4, 2, 1)


def attention(sink_ids, bias, query_rows, sink_pool, arrived, col_start):
    rows = query_rows.shape[0]
    width = arrived.shape[-1]
    block_len = arrived.shape[2]
    owners = arrived.shape[0]
    pooled = NSINK + owners
    heads = width // HS
    group = next(g for g in GROUPS if heads % g == 0)
    span = group * HS
    inv_scale = 1.0 / math.sqrt(HS)

    def kernel(slot_ref, bias_ref, q_ref, *refs):
        key_refs = refs[:pooled]
        value_refs = refs[pooled : 2 * pooled]
        out_ref = refs[2 * pooled]
        mask = bias_ref[...]
        for h in range(group):
            cols = slice(h * HS, (h + 1) * HS)
            keys = jnp.concatenate([r[:, cols] for r in key_refs], axis=0)
            values = jnp.concatenate([r[:, cols] for r in value_refs], axis=0)
            s = lax.dot_general(
                q_ref[:, cols], keys, (((1,), (1,)), ((), ())), preferred_element_type=jnp.float32
            )
            s = s * inv_scale + mask
            row_max = s.max(axis=1, keepdims=True)
            e = jnp.exp(s - row_max)
            inv_total = 1.0 / e.sum(axis=1, keepdims=True)
            w = (e * inv_total).astype(jnp.bfloat16)
            out_ref[:, cols] = jnp.dot(w, values, preferred_element_type=jnp.float32).astype(
                out_ref.dtype
            )

    def sink_spec(u, kv):
        return pl.BlockSpec(
            (None, None, block_len, span),
            lambda g, slot_ref: (slot_ref[u], kv, 0, g + col_start // span),
        )

    def window_spec(r, kv):
        return pl.BlockSpec((None, None, block_len, span), lambda g, slot_ref: (r, kv, 0, g))

    in_specs = [
        pl.BlockSpec((rows, pooled * block_len), lambda g, slot_ref: (0, 0)),
        pl.BlockSpec((rows, span), lambda g, slot_ref: (0, g + col_start // span)),
    ]
    operands = [bias, query_rows]
    for kv in range(2):
        for u in range(NSINK):
            in_specs.append(sink_spec(u, kv))
            operands.append(sink_pool)
        for r in range(owners):
            in_specs.append(window_spec(r, kv))
            operands.append(arrived)
    grid_spec = pltpu.PrefetchScalarGridSpec(
        num_scalar_prefetch=1,
        grid=(heads // group,),
        in_specs=in_specs,
        out_specs=pl.BlockSpec((rows, span), lambda g, slot_ref: (0, g)),
    )
    keys_total = pooled * block_len
    cost = pl.CostEstimate(
        flops=4 * rows * keys_total * width,
        transcendentals=heads * rows * keys_total,
        bytes_accessed=2 * rows * width * 2 + 2 * keys_total * width * 2 + rows * keys_total * 4,
    )
    return pl.pallas_call(
        kernel,
        grid_spec=grid_spec,
        out_shape=jax.ShapeDtypeStruct((rows, width), jnp.bfloat16),
        compiler_params=pltpu.CompilerParams(dimension_semantics=("arbitrary",)),
        cost_estimate=cost,
    )(sink_ids, *operands)


def visibility(block_ids, limits, owners, block_len):
    tiles = block_ids.shape[0]
    sinks = block_ids[:, :NSINK]
    window = block_ids[:, NSINK:]
    match = window[:, :, None] % owners == jnp.arange(owners, dtype=jnp.int32)[None, None, :]
    held = jnp.max(jnp.where(match, window[:, :, None], -1), axis=1)
    pooled_ids = jnp.concatenate([sinks, held], axis=1)
    visible = jnp.where(
        pooled_ids >= 0, jnp.clip(limits[:, None] - pooled_ids * block_len, 0, block_len), 0
    )
    lane = jnp.arange(block_len, dtype=jnp.int32)
    seen = lane[None, None, :] < visible[:, :, None]
    bias = jnp.where(seen, 0.0, -jnp.inf).astype(jnp.float32)
    bias = bias.reshape(tiles, 1, -1)
    return jnp.broadcast_to(bias, (tiles, block_len, bias.shape[-1])).reshape(
        tiles * block_len, -1
    )


def shards(queries, kv_cache, block_lists, key_limit, out_weight, gate):
    owners = lax.axis_size("seq")
    me = lax.axis_index("seq")
    blocks = kv_cache[0, :, 0]
    block_ids = block_lists[0]
    tiles = block_ids.shape[0]
    block_len = blocks.shape[2]
    width = blocks.shape[3]
    weight = lax.all_gather(out_weight, "fsdp", axis=0, tiled=True)
    window_ids = block_ids[:, NSINK:].reshape(-1)
    lists = [window_ids]
    for shift in range(1, owners):
        lists.append(lax.ppermute(window_ids, "seq", [(s, (s + shift) % owners) for s in range(owners)]))
    by_reader = jnp.stack(lists)
    first = jnp.broadcast_to(blocks[0][None], (owners,) + blocks.shape[1:])
    by_reader, first = lax.optimization_barrier((by_reader, first))
    sink_pool = lax.all_to_all(first, "seq", split_axis=0, concat_axis=0, tiled=True)
    readers = (me - jnp.arange(owners, dtype=jnp.int32)) % owners
    readers_ids = jnp.zeros_like(by_reader).at[readers].set(by_reader)
    asked = jnp.max(jnp.where(readers_ids % owners == me, readers_ids, -1), axis=1)
    asked_slot = jnp.minimum(jnp.maximum(asked, 0) // owners, blocks.shape[0] - 1)
    bias = visibility(block_ids, key_limit[0], owners, block_len)
    heads = width // HS
    tail_heads = heads // 4 if heads % 20 == 0 else heads
    bounds = [(0, heads - tail_heads), (heads - tail_heads, heads)]
    bounds = [(lo * HS, hi * HS) for lo, hi in bounds if hi > lo]
    projected = None
    for lo, hi in bounds:
        cols = slice(lo, hi)
        outgoing = jnp.take(blocks[..., cols], asked_slot, axis=0, mode="clip")
        if lo == 0:
            outgoing, sink_pool = lax.optimization_barrier((outgoing, sink_pool))
        arrived = lax.all_to_all(outgoing, "seq", split_axis=0, concat_axis=0, tiled=True)
        if projected is not None:
            projected, arrived = lax.optimization_barrier((projected, arrived))
        mixed = attention(block_ids[0, :NSINK], bias, queries[0], sink_pool, arrived, lo)
        part = jnp.dot(mixed, weight[cols], preferred_element_type=jnp.float32)
        projected = part if projected is None else projected + part
    return (gate[0][None, :] * projected).astype(jnp.bfloat16)[None]


def solution(mesh):
    in_specs = (
        P("fsdp", "seq", None),
        P("fsdp", None, "seq", None, None, None),
        P("fsdp", "seq", None),
        P("fsdp", "seq"),
        P("fsdp", None),
        P("fsdp", None),
    )
    out_specs = P("fsdp", "seq", None)
    return jax.shard_map(shards, mesh=mesh, in_specs=in_specs, out_specs=out_specs, check_vma=False)
```

```python
import math

import jax
import jax.numpy as jnp
from jax import lax
from jax.experimental import pallas as pl
from jax.experimental.pallas import tpu as pltpu
from jax.sharding import PartitionSpec as P

HS = 128
NSINK = 2
GROUPS = (5, 4, 2, 1)


def attention(sink_ids, bias, query_rows, sink_pool, arrived, col_start):
    rows = query_rows.shape[0]
    width = arrived.shape[-1]
    block_len = arrived.shape[2]
    owners = arrived.shape[0]
    pooled = NSINK + owners
    heads = width // HS
    group = next(g for g in GROUPS if heads % g == 0)
    span = group * HS
    inv_scale = 1.0 / math.sqrt(HS)

    def kernel(slot_ref, bias_ref, q_ref, *refs):
        key_refs = refs[:pooled]
        value_refs = refs[pooled : 2 * pooled]
        out_ref = refs[2 * pooled]
        mask = bias_ref[...]
        for h in range(group):
            cols = slice(h * HS, (h + 1) * HS)
            keys = jnp.concatenate([r[:, cols] for r in key_refs], axis=0)
            values = jnp.concatenate([r[:, cols] for r in value_refs], axis=0)
            s = lax.dot_general(
                q_ref[:, cols], keys, (((1,), (1,)), ((), ())), preferred_element_type=jnp.float32
            )
            s = s * inv_scale + mask
            row_max = s.max(axis=1, keepdims=True)
            e = jnp.exp(s - row_max)
            inv_total = 1.0 / e.sum(axis=1, keepdims=True)
            w = (e * inv_total).astype(jnp.bfloat16)
            out_ref[:, cols] = jnp.dot(w, values, preferred_element_type=jnp.float32).astype(
                out_ref.dtype
            )

    def sink_spec(u, kv):
        return pl.BlockSpec(
            (None, None, block_len, span),
            lambda g, slot_ref: (slot_ref[u], kv, 0, g + col_start // span),
        )

    def window_spec(r, kv):
        return pl.BlockSpec((None, None, block_len, span), lambda g, slot_ref: (r, kv, 0, g))

    in_specs = [
        pl.BlockSpec((rows, pooled * block_len), lambda g, slot_ref: (0, 0)),
        pl.BlockSpec((rows, span), lambda g, slot_ref: (0, g + col_start // span)),
    ]
    operands = [bias, query_rows]
    for kv in range(2):
        for u in range(NSINK):
            in_specs.append(sink_spec(u, kv))
            operands.append(sink_pool)
        for r in range(owners):
            in_specs.append(window_spec(r, kv))
            operands.append(arrived)
    grid_spec = pltpu.PrefetchScalarGridSpec(
        num_scalar_prefetch=1,
        grid=(heads // group,),
        in_specs=in_specs,
        out_specs=pl.BlockSpec((rows, span), lambda g, slot_ref: (0, g)),
    )
    keys_total = pooled * block_len
    cost = pl.CostEstimate(
        flops=4 * rows * keys_total * width,
        transcendentals=heads * rows * keys_total,
        bytes_accessed=2 * rows * width * 2 + 2 * keys_total * width * 2 + rows * keys_total * 4,
    )
    return pl.pallas_call(
        kernel,
        grid_spec=grid_spec,
        out_shape=jax.ShapeDtypeStruct((rows, width), jnp.bfloat16),
        compiler_params=pltpu.CompilerParams(dimension_semantics=("arbitrary",)),
        cost_estimate=cost,
    )(sink_ids, *operands)


def visibility(block_ids, limits, owners, block_len):
    tiles = block_ids.shape[0]
    sinks = block_ids[:, :NSINK]
    window = block_ids[:, NSINK:]
    match = window[:, :, None] % owners == jnp.arange(owners, dtype=jnp.int32)[None, None, :]
    held = jnp.max(jnp.where(match, window[:, :, None], -1), axis=1)
    pooled_ids = jnp.concatenate([sinks, held], axis=1)
    visible = jnp.where(
        pooled_ids >= 0, jnp.clip(limits[:, None] - pooled_ids * block_len, 0, block_len), 0
    )
    lane = jnp.arange(block_len, dtype=jnp.int32)
    seen = lane[None, None, :] < visible[:, :, None]
    bias = jnp.where(seen, 0.0, -jnp.inf).astype(jnp.float32)
    bias = bias.reshape(tiles, 1, -1)
    return jnp.broadcast_to(bias, (tiles, block_len, bias.shape[-1])).reshape(
        tiles * block_len, -1
    )


def shards(queries, kv_cache, block_lists, key_limit, out_weight, gate):
    owners = lax.axis_size("seq")
    me = lax.axis_index("seq")
    blocks = kv_cache[0, :, 0]
    block_ids = block_lists[0]
    tiles = block_ids.shape[0]
    block_len = blocks.shape[2]
    width = blocks.shape[3]
    weight = lax.all_gather(out_weight, "fsdp", axis=0, tiled=True)
    window_ids = block_ids[:, NSINK:].reshape(-1)
    lists = [window_ids]
    for shift in range(1, owners):
        lists.append(lax.ppermute(window_ids, "seq", [(s, (s + shift) % owners) for s in range(owners)]))
    by_reader = jnp.stack(lists)
    first = jnp.broadcast_to(blocks[0][None], (owners,) + blocks.shape[1:])
    by_reader, first = lax.optimization_barrier((by_reader, first))
    sink_pool = lax.all_to_all(first, "seq", split_axis=0, concat_axis=0, tiled=True)
    readers = (me - jnp.arange(owners, dtype=jnp.int32)) % owners
    readers_ids = jnp.zeros_like(by_reader).at[readers].set(by_reader)
    asked = jnp.max(jnp.where(readers_ids % owners == me, readers_ids, -1), axis=1)
    asked_slot = jnp.minimum(jnp.maximum(asked, 0) // owners, blocks.shape[0] - 1)
    bias = visibility(block_ids, key_limit[0], owners, block_len)
    heads = width // HS
    tail_heads = heads * 2 // 5 if heads % 5 == 0 else heads
    bounds = [(0, heads - tail_heads), (heads - tail_heads, heads)]
    bounds = [(lo * HS, hi * HS) for lo, hi in bounds if hi > lo]
    projected = None
    for lo, hi in bounds:
        cols = slice(lo, hi)
        outgoing = jnp.take(blocks[..., cols], asked_slot, axis=0, mode="clip")
        if lo == 0:
            outgoing, sink_pool = lax.optimization_barrier((outgoing, sink_pool))
        arrived = lax.all_to_all(outgoing, "seq", split_axis=0, concat_axis=0, tiled=True)
        if projected is not None:
            projected, arrived = lax.optimization_barrier((projected, arrived))
        mixed = attention(block_ids[0, :NSINK], bias, queries[0], sink_pool, arrived, lo)
        part = jnp.dot(mixed, weight[cols], preferred_element_type=jnp.float32)
        projected = part if projected is None else projected + part
    return (gate[0][None, :] * projected).astype(jnp.bfloat16)[None]


def solution(mesh):
    in_specs = (
        P("fsdp", "seq", None),
        P("fsdp", None, "seq", None, None, None),
        P("fsdp", "seq", None),
        P("fsdp", "seq"),
        P("fsdp", None),
        P("fsdp", None),
    )
    out_specs = P("fsdp", "seq", None)
    return jax.shard_map(shards, mesh=mesh, in_specs=in_specs, out_specs=out_specs, check_vma=False)
```

```python
import math

import jax
import jax.numpy as jnp
from jax import lax
from jax.experimental import pallas as pl
from jax.experimental.pallas import tpu as pltpu
from jax.sharding import PartitionSpec as P

HS = 128
NSINK = 2
GROUPS = (5, 4, 2, 1)


def attention(sink_ids, bias, query_rows, sink_pool, arrived, col_start):
    rows = query_rows.shape[0]
    width = arrived.shape[-1]
    block_len = arrived.shape[2]
    owners = arrived.shape[0]
    pooled = NSINK + owners
    heads = width // HS
    group = next(g for g in GROUPS if heads % g == 0)
    span = group * HS
    inv_scale = 1.0 / math.sqrt(HS)

    def kernel(slot_ref, bias_ref, q_ref, *refs):
        key_refs = refs[:pooled]
        value_refs = refs[pooled : 2 * pooled]
        out_ref = refs[2 * pooled]
        mask = bias_ref[...]
        for h in range(group):
            cols = slice(h * HS, (h + 1) * HS)
            keys = jnp.concatenate([r[:, cols] for r in key_refs], axis=0)
            values = jnp.concatenate([r[:, cols] for r in value_refs], axis=0)
            s = lax.dot_general(
                q_ref[:, cols], keys, (((1,), (1,)), ((), ())), preferred_element_type=jnp.float32
            )
            s = s * inv_scale + mask
            row_max = s.max(axis=1, keepdims=True)
            e = jnp.exp(s - row_max)
            inv_total = 1.0 / e.sum(axis=1, keepdims=True)
            w = (e * inv_total).astype(jnp.bfloat16)
            out_ref[:, cols] = jnp.dot(w, values, preferred_element_type=jnp.float32).astype(
                out_ref.dtype
            )

    def sink_spec(u, kv):
        return pl.BlockSpec(
            (None, None, block_len, span),
            lambda g, slot_ref: (slot_ref[u], kv, 0, g + col_start // span),
        )

    def window_spec(r, kv):
        return pl.BlockSpec((None, None, block_len, span), lambda g, slot_ref: (r, kv, 0, g))

    in_specs = [
        pl.BlockSpec((rows, pooled * block_len), lambda g, slot_ref: (0, 0)),
        pl.BlockSpec((rows, span), lambda g, slot_ref: (0, g + col_start // span)),
    ]
    operands = [bias, query_rows]
    for kv in range(2):
        for u in range(NSINK):
            in_specs.append(sink_spec(u, kv))
            operands.append(sink_pool)
        for r in range(owners):
            in_specs.append(window_spec(r, kv))
            operands.append(arrived)
    grid_spec = pltpu.PrefetchScalarGridSpec(
        num_scalar_prefetch=1,
        grid=(heads // group,),
        in_specs=in_specs,
        out_specs=pl.BlockSpec((rows, span), lambda g, slot_ref: (0, g)),
    )
    keys_total = pooled * block_len
    cost = pl.CostEstimate(
        flops=4 * rows * keys_total * width,
        transcendentals=heads * rows * keys_total,
        bytes_accessed=2 * rows * width * 2 + 2 * keys_total * width * 2 + rows * keys_total * 4,
    )
    return pl.pallas_call(
        kernel,
        grid_spec=grid_spec,
        out_shape=jax.ShapeDtypeStruct((rows, width), jnp.bfloat16),
        compiler_params=pltpu.CompilerParams(dimension_semantics=("arbitrary",)),
        cost_estimate=cost,
    )(sink_ids, *operands)


def visibility(block_ids, limits, owners, block_len):
    tiles = block_ids.shape[0]
    sinks = block_ids[:, :NSINK]
    window = block_ids[:, NSINK:]
    match = window[:, :, None] % owners == jnp.arange(owners, dtype=jnp.int32)[None, None, :]
    held = jnp.max(jnp.where(match, window[:, :, None], -1), axis=1)
    pooled_ids = jnp.concatenate([sinks, held], axis=1)
    visible = jnp.where(
        pooled_ids >= 0, jnp.clip(limits[:, None] - pooled_ids * block_len, 0, block_len), 0
    )
    lane = jnp.arange(block_len, dtype=jnp.int32)
    seen = lane[None, None, :] < visible[:, :, None]
    bias = jnp.where(seen, 0.0, -jnp.inf).astype(jnp.float32)
    bias = bias.reshape(tiles, 1, -1)
    return jnp.broadcast_to(bias, (tiles, block_len, bias.shape[-1])).reshape(
        tiles * block_len, -1
    )


def shards(queries, kv_cache, block_lists, key_limit, out_weight, gate):
    owners = lax.axis_size("seq")
    me = lax.axis_index("seq")
    blocks = kv_cache[0, :, 0]
    block_ids = block_lists[0]
    tiles = block_ids.shape[0]
    block_len = blocks.shape[2]
    width = blocks.shape[3]
    weight = lax.all_gather(out_weight, "fsdp", axis=0, tiled=True)
    window_ids = block_ids[:, NSINK:].reshape(-1)
    lists = [window_ids]
    for shift in range(1, owners):
        lists.append(lax.ppermute(window_ids, "seq", [(s, (s + shift) % owners) for s in range(owners)]))
    by_reader = jnp.stack(lists)
    first = jnp.broadcast_to(blocks[0][None], (owners,) + blocks.shape[1:])
    sink_pool = lax.all_to_all(first, "seq", split_axis=0, concat_axis=0, tiled=True)
    readers = (me - jnp.arange(owners, dtype=jnp.int32)) % owners
    readers_ids = jnp.zeros_like(by_reader).at[readers].set(by_reader)
    asked = jnp.max(jnp.where(readers_ids % owners == me, readers_ids, -1), axis=1)
    asked_slot = jnp.minimum(jnp.maximum(asked, 0) // owners, blocks.shape[0] - 1)
    bias = visibility(block_ids, key_limit[0], owners, block_len)
    heads = width // HS
    tail_heads = heads * 2 // 5 if heads % 5 == 0 else heads
    bounds = [(0, heads - tail_heads), (heads - tail_heads, heads)]
    bounds = [(lo * HS, hi * HS) for lo, hi in bounds if hi > lo]
    projected = None
    for lo, hi in bounds:
        cols = slice(lo, hi)
        outgoing = jnp.take(blocks[..., cols], asked_slot, axis=0, mode="clip")
        if lo == 0:
            outgoing, sink_pool = lax.optimization_barrier((outgoing, sink_pool))
        arrived = lax.all_to_all(outgoing, "seq", split_axis=0, concat_axis=0, tiled=True)
        if projected is not None:
            projected, arrived = lax.optimization_barrier((projected, arrived))
        mixed = attention(block_ids[0, :NSINK], bias, queries[0], sink_pool, arrived, lo)
        part = jnp.dot(mixed, weight[cols], preferred_element_type=jnp.float32)
        projected = part if projected is None else projected + part
    return (gate[0][None, :] * projected).astype(jnp.bfloat16)[None]


def solution(mesh):
    in_specs = (
        P("fsdp", "seq", None),
        P("fsdp", None, "seq", None, None, None),
        P("fsdp", "seq", None),
        P("fsdp", "seq"),
        P("fsdp", None),
        P("fsdp", None),
    )
    out_specs = P("fsdp", "seq", None)
    return jax.shard_map(shards, mesh=mesh, in_specs=in_specs, out_specs=out_specs, check_vma=False)
```

```python
import math

import jax
import jax.numpy as jnp
from jax import lax
from jax.experimental import pallas as pl
from jax.experimental.pallas import tpu as pltpu
from jax.sharding import PartitionSpec as P

HS = 128
NSINK = 2
GROUPS = (5, 4, 2, 1)


def attention(sink_ids, bias, query_rows, arrived, col_start):
    rows = query_rows.shape[0]
    width = arrived.shape[-1]
    block_len = arrived.shape[3]
    owners = arrived.shape[0]
    pooled = NSINK + owners
    heads = width // HS
    group = next(g for g in GROUPS if heads % g == 0)
    span = group * HS
    inv_scale = 1.0 / math.sqrt(HS)

    def kernel(slot_ref, bias_ref, q_ref, *refs):
        key_refs = refs[:pooled]
        value_refs = refs[pooled : 2 * pooled]
        out_ref = refs[2 * pooled]
        mask = bias_ref[...]
        for h in range(group):
            cols = slice(h * HS, (h + 1) * HS)
            keys = jnp.concatenate([r[:, cols] for r in key_refs], axis=0)
            values = jnp.concatenate([r[:, cols] for r in value_refs], axis=0)
            s = lax.dot_general(
                q_ref[:, cols], keys, (((1,), (1,)), ((), ())), preferred_element_type=jnp.float32
            )
            s = s * inv_scale + mask
            row_max = s.max(axis=1, keepdims=True)
            e = jnp.exp(s - row_max)
            inv_total = 1.0 / e.sum(axis=1, keepdims=True)
            w = (e * inv_total).astype(jnp.bfloat16)
            out_ref[:, cols] = jnp.dot(w, values, preferred_element_type=jnp.float32).astype(
                out_ref.dtype
            )

    def sink_spec(u, kv):
        return pl.BlockSpec(
            (None, None, None, block_len, span), lambda g, slot_ref: (slot_ref[u], 1, kv, 0, g)
        )

    def window_spec(r, kv):
        return pl.BlockSpec(
            (None, None, None, block_len, span), lambda g, slot_ref: (r, 0, kv, 0, g)
        )

    in_specs = [
        pl.BlockSpec((rows, pooled * block_len), lambda g, slot_ref: (0, 0)),
        pl.BlockSpec((rows, span), lambda g, slot_ref: (0, g + col_start // span)),
    ]
    operands = [bias, query_rows]
    for kv in range(2):
        for u in range(NSINK):
            in_specs.append(sink_spec(u, kv))
            operands.append(arrived)
        for r in range(owners):
            in_specs.append(window_spec(r, kv))
            operands.append(arrived)
    grid_spec = pltpu.PrefetchScalarGridSpec(
        num_scalar_prefetch=1,
        grid=(heads // group,),
        in_specs=in_specs,
        out_specs=pl.BlockSpec((rows, span), lambda g, slot_ref: (0, g)),
    )
    keys_total = pooled * block_len
    cost = pl.CostEstimate(
        flops=4 * rows * keys_total * width,
        transcendentals=heads * rows * keys_total,
        bytes_accessed=2 * rows * width * 2 + 2 * keys_total * width * 2 + rows * keys_total * 4,
    )
    return pl.pallas_call(
        kernel,
        grid_spec=grid_spec,
        out_shape=jax.ShapeDtypeStruct((rows, width), jnp.bfloat16),
        compiler_params=pltpu.CompilerParams(dimension_semantics=("arbitrary",)),
        cost_estimate=cost,
    )(sink_ids, *operands)


def visibility(block_ids, limits, owners, block_len):
    tiles = block_ids.shape[0]
    sinks = block_ids[:, :NSINK]
    window = block_ids[:, NSINK:]
    match = window[:, :, None] % owners == jnp.arange(owners, dtype=jnp.int32)[None, None, :]
    held = jnp.max(jnp.where(match, window[:, :, None], -1), axis=1)
    pooled_ids = jnp.concatenate([sinks, held], axis=1)
    visible = jnp.where(
        pooled_ids >= 0, jnp.clip(limits[:, None] - pooled_ids * block_len, 0, block_len), 0
    )
    lane = jnp.arange(block_len, dtype=jnp.int32)
    seen = lane[None, None, :] < visible[:, :, None]
    bias = jnp.where(seen, 0.0, -jnp.inf).astype(jnp.float32)
    bias = bias.reshape(tiles, 1, -1)
    return jnp.broadcast_to(bias, (tiles, block_len, bias.shape[-1])).reshape(
        tiles * block_len, -1
    )


def shards(queries, kv_cache, block_lists, key_limit, out_weight, gate):
    owners = lax.axis_size("seq")
    me = lax.axis_index("seq")
    blocks = kv_cache[0, :, 0]
    block_ids = block_lists[0]
    tiles = block_ids.shape[0]
    block_len = blocks.shape[2]
    width = blocks.shape[3]
    weight = lax.all_gather(out_weight, "fsdp", axis=0, tiled=True)
    window_ids = block_ids[:, NSINK:].reshape(-1)
    lists = [window_ids]
    for shift in range(1, owners):
        lists.append(lax.ppermute(window_ids, "seq", [(s, (s + shift) % owners) for s in range(owners)]))
    by_reader = jnp.stack(lists)
    readers = (me - jnp.arange(owners, dtype=jnp.int32)) % owners
    readers_ids = jnp.zeros_like(by_reader).at[readers].set(by_reader)
    asked = jnp.max(jnp.where(readers_ids % owners == me, readers_ids, -1), axis=1)
    asked_slot = jnp.minimum(jnp.maximum(asked, 0) // owners, blocks.shape[0] - 1)
    picks = jnp.stack([asked_slot, jnp.zeros_like(asked_slot)], axis=1).reshape(-1)
    bias = visibility(block_ids, key_limit[0], owners, block_len)
    heads = width // HS
    if heads % 20 == 0:
        edges = [0, heads // 5, heads * 4 // 5, heads]
    else:
        edges = [0, heads]
    bounds = [(lo * HS, hi * HS) for lo, hi in zip(edges[:-1], edges[1:])]
    projected = None
    for lo, hi in bounds:
        cols = slice(lo, hi)
        outgoing = jnp.take(blocks[..., cols], picks, axis=0, mode="clip")
        outgoing = outgoing.reshape(owners, 2, 2, block_len, hi - lo)
        if lo > 0:
            previous, outgoing = lax.optimization_barrier((previous, outgoing))
        arrived = lax.all_to_all(outgoing, "seq", split_axis=0, concat_axis=0, tiled=True)
        previous = arrived
        if hi == bounds[-1][1] and projected is not None:
            projected, arrived = lax.optimization_barrier((projected, arrived))
        mixed = attention(block_ids[0, :NSINK], bias, queries[0], arrived, lo)
        part = jnp.dot(mixed, weight[cols], preferred_element_type=jnp.float32)
        projected = part if projected is None else projected + part
    return (gate[0][None, :] * projected).astype(jnp.bfloat16)[None]


def solution(mesh):
    in_specs = (
        P("fsdp", "seq", None),
        P("fsdp", None, "seq", None, None, None),
        P("fsdp", "seq", None),
        P("fsdp", "seq"),
        P("fsdp", None),
        P("fsdp", None),
    )
    out_specs = P("fsdp", "seq", None)
    return jax.shard_map(shards, mesh=mesh, in_specs=in_specs, out_specs=out_specs, check_vma=False)
```

```python
import math

import jax
import jax.numpy as jnp
from jax import lax
from jax.experimental import pallas as pl
from jax.experimental.pallas import tpu as pltpu
from jax.sharding import PartitionSpec as P

HS = 128
NSINK = 2
GROUPS = (5, 4, 2, 1)


def attention(sink_ids, bias, query_rows, arrived, col_start):
    rows = query_rows.shape[0]
    width = arrived.shape[-1]
    block_len = arrived.shape[3]
    owners = arrived.shape[0]
    pooled = NSINK + owners
    heads = width // HS
    group = next(g for g in GROUPS if heads % g == 0 and (heads // g > 1 or g == 1))
    span = group * HS
    inv_scale = 1.0 / math.sqrt(HS)

    def kernel(slot_ref, bias_ref, q_ref, *refs):
        key_refs = refs[:pooled]
        value_refs = refs[pooled : 2 * pooled]
        out_ref = refs[2 * pooled]
        mask = bias_ref[...]
        for h in range(group):
            cols = slice(h * HS, (h + 1) * HS)
            keys = jnp.concatenate([r[:, cols] for r in key_refs], axis=0)
            values = jnp.concatenate([r[:, cols] for r in value_refs], axis=0)
            s = lax.dot_general(
                q_ref[:, cols], keys, (((1,), (1,)), ((), ())), preferred_element_type=jnp.float32
            )
            s = s * inv_scale + mask
            row_max = s.max(axis=1, keepdims=True)
            e = jnp.exp(s - row_max)
            inv_total = 1.0 / e.sum(axis=1, keepdims=True)
            w = (e * inv_total).astype(jnp.bfloat16)
            out_ref[:, cols] = jnp.dot(w, values, preferred_element_type=jnp.float32).astype(
                out_ref.dtype
            )

    def sink_spec(u, kv):
        return pl.BlockSpec(
            (None, None, None, block_len, span), lambda g, slot_ref: (slot_ref[u], 1, kv, 0, g)
        )

    def window_spec(r, kv):
        return pl.BlockSpec(
            (None, None, None, block_len, span), lambda g, slot_ref: (r, 0, kv, 0, g)
        )

    in_specs = [
        pl.BlockSpec((rows, pooled * block_len), lambda g, slot_ref: (0, 0)),
        pl.BlockSpec((rows, span), lambda g, slot_ref: (0, g + col_start // span)),
    ]
    operands = [bias, query_rows]
    for kv in range(2):
        for u in range(NSINK):
            in_specs.append(sink_spec(u, kv))
            operands.append(arrived)
        for r in range(owners):
            in_specs.append(window_spec(r, kv))
            operands.append(arrived)
    grid_spec = pltpu.PrefetchScalarGridSpec(
        num_scalar_prefetch=1,
        grid=(heads // group,),
        in_specs=in_specs,
        out_specs=pl.BlockSpec((rows, span), lambda g, slot_ref: (0, g)),
    )
    keys_total = pooled * block_len
    cost = pl.CostEstimate(
        flops=4 * rows * keys_total * width,
        transcendentals=heads * rows * keys_total,
        bytes_accessed=2 * rows * width * 2 + 2 * keys_total * width * 2 + rows * keys_total * 4,
    )
    return pl.pallas_call(
        kernel,
        grid_spec=grid_spec,
        out_shape=jax.ShapeDtypeStruct((rows, width), jnp.bfloat16),
        compiler_params=pltpu.CompilerParams(dimension_semantics=("arbitrary",)),
        cost_estimate=cost,
    )(sink_ids, *operands)


def visibility(block_ids, limits, owners, block_len):
    tiles = block_ids.shape[0]
    sinks = block_ids[:, :NSINK]
    window = block_ids[:, NSINK:]
    match = window[:, :, None] % owners == jnp.arange(owners, dtype=jnp.int32)[None, None, :]
    held = jnp.max(jnp.where(match, window[:, :, None], -1), axis=1)
    pooled_ids = jnp.concatenate([sinks, held], axis=1)
    visible = jnp.where(
        pooled_ids >= 0, jnp.clip(limits[:, None] - pooled_ids * block_len, 0, block_len), 0
    )
    lane = jnp.arange(block_len, dtype=jnp.int32)
    seen = lane[None, None, :] < visible[:, :, None]
    bias = jnp.where(seen, 0.0, -jnp.inf).astype(jnp.float32)
    bias = bias.reshape(tiles, 1, -1)
    return jnp.broadcast_to(bias, (tiles, block_len, bias.shape[-1])).reshape(
        tiles * block_len, -1
    )


def shards(queries, kv_cache, block_lists, key_limit, out_weight, gate):
    owners = lax.axis_size("seq")
    me = lax.axis_index("seq")
    blocks = kv_cache[0, :, 0]
    block_ids = block_lists[0]
    tiles = block_ids.shape[0]
    block_len = blocks.shape[2]
    width = blocks.shape[3]
    weight = lax.all_gather(out_weight, "fsdp", axis=0, tiled=True)
    window_ids = block_ids[:, NSINK:].reshape(-1)
    lists = [window_ids]
    for shift in range(1, owners):
        lists.append(lax.ppermute(window_ids, "seq", [(s, (s + shift) % owners) for s in range(owners)]))
    by_reader = jnp.stack(lists)
    readers = (me - jnp.arange(owners, dtype=jnp.int32)) % owners
    readers_ids = jnp.zeros_like(by_reader).at[readers].set(by_reader)
    asked = jnp.max(jnp.where(readers_ids % owners == me, readers_ids, -1), axis=1)
    asked_slot = jnp.minimum(jnp.maximum(asked, 0) // owners, blocks.shape[0] - 1)
    picks = jnp.stack([asked_slot, jnp.zeros_like(asked_slot)], axis=1).reshape(-1)
    bias = visibility(block_ids, key_limit[0], owners, block_len)
    heads = width // HS
    if heads % 20 == 0:
        edges = [0, heads // 5, heads * 4 // 5, heads]
    else:
        edges = [0, heads]
    bounds = [(lo * HS, hi * HS) for lo, hi in zip(edges[:-1], edges[1:])]
    projected = None
    for lo, hi in bounds:
        cols = slice(lo, hi)
        outgoing = jnp.take(blocks[..., cols], picks, axis=0, mode="clip")
        outgoing = outgoing.reshape(owners, 2, 2, block_len, hi - lo)
        if lo > 0:
            previous, outgoing = lax.optimization_barrier((previous, outgoing))
        arrived = lax.all_to_all(outgoing, "seq", split_axis=0, concat_axis=0, tiled=True)
        previous = arrived
        if hi == bounds[-1][1] and projected is not None:
            projected, arrived = lax.optimization_barrier((projected, arrived))
        mixed = attention(block_ids[0, :NSINK], bias, queries[0], arrived, lo)
        part = jnp.dot(mixed, weight[cols], preferred_element_type=jnp.float32)
        projected = part if projected is None else projected + part
    return (gate[0][None, :] * projected).astype(jnp.bfloat16)[None]


def solution(mesh):
    in_specs = (
        P("fsdp", "seq", None),
        P("fsdp", None, "seq", None, None, None),
        P("fsdp", "seq", None),
        P("fsdp", "seq"),
        P("fsdp", None),
        P("fsdp", None),
    )
    out_specs = P("fsdp", "seq", None)
    return jax.shard_map(shards, mesh=mesh, in_specs=in_specs, out_specs=out_specs, check_vma=False)
```

```python
import math

import jax
import jax.numpy as jnp
from jax import lax
from jax.experimental import pallas as pl
from jax.experimental.pallas import tpu as pltpu
from jax.sharding import PartitionSpec as P

HS = 128
NSINK = 2
GROUPS = (5, 4, 2, 1)


def attention(sink_ids, bias, query_rows, arrived, col_start):
    rows = query_rows.shape[0]
    width = arrived.shape[-1]
    block_len = arrived.shape[3]
    owners = arrived.shape[0]
    pooled = NSINK + owners
    heads = width // HS
    group = next(g for g in GROUPS if heads % g == 0)
    span = group * HS
    inv_scale = 1.0 / math.sqrt(HS)

    def kernel(slot_ref, bias_ref, q_ref, *refs):
        key_refs = refs[:pooled]
        value_refs = refs[pooled : 2 * pooled]
        out_ref = refs[2 * pooled]
        mask = bias_ref[...]
        for h in range(group):
            cols = slice(h * HS, (h + 1) * HS)
            keys = jnp.concatenate([r[:, cols] for r in key_refs], axis=0)
            values = jnp.concatenate([r[:, cols] for r in value_refs], axis=0)
            s = lax.dot_general(
                q_ref[:, cols], keys, (((1,), (1,)), ((), ())), preferred_element_type=jnp.float32
            )
            s = s * inv_scale + mask
            row_max = s.max(axis=1, keepdims=True)
            e = jnp.exp(s - row_max)
            inv_total = 1.0 / e.sum(axis=1, keepdims=True)
            w = (e * inv_total).astype(jnp.bfloat16)
            out_ref[:, cols] = jnp.dot(w, values, preferred_element_type=jnp.float32).astype(
                out_ref.dtype
            )

    def sink_spec(u, kv):
        return pl.BlockSpec(
            (None, None, None, block_len, span), lambda g, slot_ref: (slot_ref[u], 1, kv, 0, g)
        )

    def window_spec(r, kv):
        return pl.BlockSpec(
            (None, None, None, block_len, span), lambda g, slot_ref: (r, 0, kv, 0, g)
        )

    in_specs = [
        pl.BlockSpec((rows, pooled * block_len), lambda g, slot_ref: (0, 0)),
        pl.BlockSpec((rows, span), lambda g, slot_ref: (0, g + col_start // span)),
    ]
    operands = [bias, query_rows]
    for kv in range(2):
        for u in range(NSINK):
            in_specs.append(sink_spec(u, kv))
            operands.append(arrived)
        for r in range(owners):
            in_specs.append(window_spec(r, kv))
            operands.append(arrived)
    grid_spec = pltpu.PrefetchScalarGridSpec(
        num_scalar_prefetch=1,
        grid=(heads // group,),
        in_specs=in_specs,
        out_specs=pl.BlockSpec((rows, span), lambda g, slot_ref: (0, g)),
    )
    keys_total = pooled * block_len
    cost = pl.CostEstimate(
        flops=4 * rows * keys_total * width,
        transcendentals=heads * rows * keys_total,
        bytes_accessed=2 * rows * width * 2 + 2 * keys_total * width * 2 + rows * keys_total * 4,
    )
    return pl.pallas_call(
        kernel,
        grid_spec=grid_spec,
        out_shape=jax.ShapeDtypeStruct((rows, width), jnp.bfloat16),
        compiler_params=pltpu.CompilerParams(dimension_semantics=("arbitrary",)),
        cost_estimate=cost,
    )(sink_ids, *operands)


def visibility(block_ids, limits, owners, block_len):
    tiles = block_ids.shape[0]
    sinks = block_ids[:, :NSINK]
    window = block_ids[:, NSINK:]
    match = window[:, :, None] % owners == jnp.arange(owners, dtype=jnp.int32)[None, None, :]
    held = jnp.max(jnp.where(match, window[:, :, None], -1), axis=1)
    pooled_ids = jnp.concatenate([sinks, held], axis=1)
    visible = jnp.where(
        pooled_ids >= 0, jnp.clip(limits[:, None] - pooled_ids * block_len, 0, block_len), 0
    )
    lane = jnp.arange(block_len, dtype=jnp.int32)
    seen = lane[None, None, :] < visible[:, :, None]
    bias = jnp.where(seen, 0.0, -jnp.inf).astype(jnp.float32)
    bias = bias.reshape(tiles, 1, -1)
    return jnp.broadcast_to(bias, (tiles, block_len, bias.shape[-1])).reshape(
        tiles * block_len, -1
    )


def shards(queries, kv_cache, block_lists, key_limit, out_weight, gate):
    owners = lax.axis_size("seq")
    me = lax.axis_index("seq")
    blocks = kv_cache[0, :, 0]
    block_ids = block_lists[0]
    tiles = block_ids.shape[0]
    block_len = blocks.shape[2]
    width = blocks.shape[3]
    weight = lax.all_gather(out_weight, "fsdp", axis=0, tiled=True)
    window_ids = block_ids[:, NSINK:].reshape(-1)
    lists = [window_ids]
    for shift in range(1, owners):
        lists.append(lax.ppermute(window_ids, "seq", [(s, (s + shift) % owners) for s in range(owners)]))
    by_reader = jnp.stack(lists)
    readers = (me - jnp.arange(owners, dtype=jnp.int32)) % owners
    readers_ids = jnp.zeros_like(by_reader).at[readers].set(by_reader)
    asked = jnp.max(jnp.where(readers_ids % owners == me, readers_ids, -1), axis=1)
    asked_slot = jnp.minimum(jnp.maximum(asked, 0) // owners, blocks.shape[0] - 1)
    picks = jnp.stack([asked_slot, jnp.zeros_like(asked_slot)], axis=1).reshape(-1)
    bias = visibility(block_ids, key_limit[0], owners, block_len)
    heads = width // HS
    if heads % 20 == 0:
        edges = [0, heads // 10, heads * 4 // 5, heads]
    else:
        edges = [0, heads]
    bounds = [(lo * HS, hi * HS) for lo, hi in zip(edges[:-1], edges[1:])]
    projected = None
    for lo, hi in bounds:
        cols = slice(lo, hi)
        outgoing = jnp.take(blocks[..., cols], picks, axis=0, mode="clip")
        outgoing = outgoing.reshape(owners, 2, 2, block_len, hi - lo)
        if lo > 0:
            previous, outgoing = lax.optimization_barrier((previous, outgoing))
        arrived = lax.all_to_all(outgoing, "seq", split_axis=0, concat_axis=0, tiled=True)
        previous = arrived
        if hi == bounds[-1][1] and projected is not None:
            projected, arrived = lax.optimization_barrier((projected, arrived))
        mixed = attention(block_ids[0, :NSINK], bias, queries[0], arrived, lo)
        part = jnp.dot(mixed, weight[cols], preferred_element_type=jnp.float32)
        projected = part if projected is None else projected + part
    return (gate[0][None, :] * projected).astype(jnp.bfloat16)[None]


def solution(mesh):
    in_specs = (
        P("fsdp", "seq", None),
        P("fsdp", None, "seq", None, None, None),
        P("fsdp", "seq", None),
        P("fsdp", "seq"),
        P("fsdp", None),
        P("fsdp", None),
    )
    out_specs = P("fsdp", "seq", None)
    return jax.shard_map(shards, mesh=mesh, in_specs=in_specs, out_specs=out_specs, check_vma=False)
```

```python
import math

import jax
import jax.numpy as jnp
from jax import lax
from jax.experimental import pallas as pl
from jax.experimental.pallas import tpu as pltpu
from jax.sharding import PartitionSpec as P

HS = 128
NSINK = 2
GROUPS = (5, 4, 2, 1)


def attention(sink_ids, bias, query_rows, arrived, col_start):
    rows = query_rows.shape[0]
    width = arrived.shape[-1]
    block_len = arrived.shape[3]
    owners = arrived.shape[0]
    pooled = NSINK + owners
    heads = width // HS
    group = next(g for g in GROUPS if heads % g == 0)
    span = group * HS
    inv_scale = 1.0 / math.sqrt(HS)

    def kernel(slot_ref, bias_ref, q_ref, *refs):
        key_refs = refs[:pooled]
        value_refs = refs[pooled : 2 * pooled]
        out_ref = refs[2 * pooled]
        mask = bias_ref[...].astype(jnp.float32)
        for h in range(group):
            cols = slice(h * HS, (h + 1) * HS)
            keys = jnp.concatenate([r[:, cols] for r in key_refs], axis=0)
            values = jnp.concatenate([r[:, cols] for r in value_refs], axis=0)
            s = lax.dot_general(
                q_ref[:, cols], keys, (((1,), (1,)), ((), ())), preferred_element_type=jnp.float32
            )
            s = s * inv_scale + mask
            row_max = s.max(axis=1, keepdims=True)
            e = jnp.exp(s - row_max)
            inv_total = 1.0 / e.sum(axis=1, keepdims=True)
            w = (e * inv_total).astype(jnp.bfloat16)
            out_ref[:, cols] = jnp.dot(w, values, preferred_element_type=jnp.float32).astype(
                out_ref.dtype
            )

    def sink_spec(u, kv):
        return pl.BlockSpec(
            (None, None, None, block_len, span), lambda g, slot_ref: (slot_ref[u], 1, kv, 0, g)
        )

    def window_spec(r, kv):
        return pl.BlockSpec(
            (None, None, None, block_len, span), lambda g, slot_ref: (r, 0, kv, 0, g)
        )

    in_specs = [
        pl.BlockSpec((rows, pooled * block_len), lambda g, slot_ref: (0, 0)),
        pl.BlockSpec((rows, span), lambda g, slot_ref: (0, g + col_start // span)),
    ]
    operands = [bias, query_rows]
    for kv in range(2):
        for u in range(NSINK):
            in_specs.append(sink_spec(u, kv))
            operands.append(arrived)
        for r in range(owners):
            in_specs.append(window_spec(r, kv))
            operands.append(arrived)
    grid_spec = pltpu.PrefetchScalarGridSpec(
        num_scalar_prefetch=1,
        grid=(heads // group,),
        in_specs=in_specs,
        out_specs=pl.BlockSpec((rows, span), lambda g, slot_ref: (0, g)),
    )
    keys_total = pooled * block_len
    cost = pl.CostEstimate(
        flops=4 * rows * keys_total * width,
        transcendentals=heads * rows * keys_total,
        bytes_accessed=2 * rows * width * 2 + 2 * keys_total * width * 2 + rows * keys_total * 2,
    )
    return pl.pallas_call(
        kernel,
        grid_spec=grid_spec,
        out_shape=jax.ShapeDtypeStruct((rows, width), jnp.bfloat16),
        compiler_params=pltpu.CompilerParams(dimension_semantics=("arbitrary",)),
        cost_estimate=cost,
    )(sink_ids, *operands)


def visibility(block_ids, limits, owners, block_len):
    tiles = block_ids.shape[0]
    sinks = block_ids[:, :NSINK]
    window = block_ids[:, NSINK:]
    match = window[:, :, None] % owners == jnp.arange(owners, dtype=jnp.int32)[None, None, :]
    held = jnp.max(jnp.where(match, window[:, :, None], -1), axis=1)
    pooled_ids = jnp.concatenate([sinks, held], axis=1)
    visible = jnp.where(
        pooled_ids >= 0, jnp.clip(limits[:, None] - pooled_ids * block_len, 0, block_len), 0
    )
    lane = jnp.arange(block_len, dtype=jnp.int32)
    seen = lane[None, None, :] < visible[:, :, None]
    bias = jnp.where(seen, 0.0, -jnp.inf).astype(jnp.bfloat16)
    bias = bias.reshape(tiles, 1, -1)
    return jnp.broadcast_to(bias, (tiles, block_len, bias.shape[-1])).reshape(
        tiles * block_len, -1
    )


def shards(queries, kv_cache, block_lists, key_limit, out_weight, gate):
    owners = lax.axis_size("seq")
    me = lax.axis_index("seq")
    blocks = kv_cache[0, :, 0]
    block_ids = block_lists[0]
    tiles = block_ids.shape[0]
    block_len = blocks.shape[2]
    width = blocks.shape[3]
    weight = lax.all_gather(out_weight, "fsdp", axis=0, tiled=True)
    window_ids = block_ids[:, NSINK:].reshape(-1)
    lists = [window_ids]
    for shift in range(1, owners):
        lists.append(lax.ppermute(window_ids, "seq", [(s, (s + shift) % owners) for s in range(owners)]))
    by_reader = jnp.stack(lists)
    readers = (me - jnp.arange(owners, dtype=jnp.int32)) % owners
    readers_ids = jnp.zeros_like(by_reader).at[readers].set(by_reader)
    asked = jnp.max(jnp.where(readers_ids % owners == me, readers_ids, -1), axis=1)
    asked_slot = jnp.minimum(jnp.maximum(asked, 0) // owners, blocks.shape[0] - 1)
    picks = jnp.stack([asked_slot, jnp.zeros_like(asked_slot)], axis=1).reshape(-1)
    bias = visibility(block_ids, key_limit[0], owners, block_len)
    heads = width // HS
    if heads % 20 == 0:
        edges = [0, heads // 5, heads * 4 // 5, heads]
    else:
        edges = [0, heads]
    bounds = [(lo * HS, hi * HS) for lo, hi in zip(edges[:-1], edges[1:])]
    projected = None
    for lo, hi in bounds:
        cols = slice(lo, hi)
        outgoing = jnp.take(blocks[..., cols], picks, axis=0, mode="clip")
        outgoing = outgoing.reshape(owners, 2, 2, block_len, hi - lo)
        if lo > 0:
            previous, outgoing = lax.optimization_barrier((previous, outgoing))
        arrived = lax.all_to_all(outgoing, "seq", split_axis=0, concat_axis=0, tiled=True)
        previous = arrived
        if hi == bounds[-1][1] and projected is not None:
            projected, arrived = lax.optimization_barrier((projected, arrived))
        mixed = attention(block_ids[0, :NSINK], bias, queries[0], arrived, lo)
        part = jnp.dot(mixed, weight[cols], preferred_element_type=jnp.float32)
        projected = part if projected is None else projected + part
    return (gate[0][None, :] * projected).astype(jnp.bfloat16)[None]


def solution(mesh):
    in_specs = (
        P("fsdp", "seq", None),
        P("fsdp", None, "seq", None, None, None),
        P("fsdp", "seq", None),
        P("fsdp", "seq"),
        P("fsdp", None),
        P("fsdp", None),
    )
    out_specs = P("fsdp", "seq", None)
    return jax.shard_map(shards, mesh=mesh, in_specs=in_specs, out_specs=out_specs, check_vma=False)
```
